256 devices in a mesh: seq: 16 (over x, y), exp: 16 (over z, core).
Axes of the slice: x: 4, y: 4, z: 8, core: 2. Of those that a mesh axis runs over, the one named last changes fastest.
Arguments:
- tokens: bfloat16 [16384, 2048], P('seq', 'exp'), may hold values from -51 to 51
- in_gain: float32 [2048], replicated, may hold values from 0.1 to 1.9
- w_query: bfloat16 [2048, 2048], P(None, 'exp'), may hold values from -0.125 to 0.125
- w_key: bfloat16 [2048, 2048], P(None, 'exp'), may hold values from -0.125 to 0.125
- w_value: bfloat16 [2048, 4096], P(None, 'exp'), may hold values from -0.125 to 0.125
- w_zgate: bfloat16 [2048, 4096], P(None, 'exp'), may hold values from -0.125 to 0.125
- conv_query: float32 [4, 2048], P(None, 'exp'), may hold values from -3 to 3
- conv_key: float32 [4, 2048], P(None, 'exp'), may hold values from -3 to 3
- conv_value: float32 [4, 4096], P(None, 'exp'), may hold values from -3 to 3
- log_decay: float32 [16384, 32], P('seq', 'exp'), may hold values from -1.7 to 0
- write_rate: float32 [16384, 32], P('seq', 'exp'), may hold values from 0 to 1
- norm_gain: float32 [128], replicated, may hold values from 0.1 to 1.9
- w_out: bfloat16 [4096, 2048], P('exp'), may hold values from -0.09375 to 0.09375
- post_gain: float32 [2048], replicated, may hold values from 0.1 to 1.9
- expert_ids: int32 [16384, 2], P(('seq', 'exp')), may hold values from 0 to 15, as said below
- route_weight: float32 [16384, 2], P(('seq', 'exp')), may hold values from 0.1 to 1
- w_gate: bfloat16 [16, 2048, 512], P('exp'), may hold values from -0.125 to 0.125
- w_up: bfloat16 [16, 2048, 512], P('exp'), may hold values from -0.125 to 0.125
- w_down: bfloat16 [16, 512, 2048], P('exp'), may hold values from -0.25 to 0.25
Outputs:
- block_out: bfloat16 [16384, 2048], P(('seq', 'exp'))
The draws below stay inside these ranges and needn't reach their ends.
Inputs may be any that keep to these rules, and one draw needn't show every extreme that they name: `expert_ids`: each row names 2 different experts. In each aligned block of 64 rows (the rows of one device) no expert is named more than 16 times, and in every aligned block of 1024 rows some expert is named exactly 16 times in each of its blocks of 64 rows.
All inputs are finite; a program needn't handle non-finite values.
Results may differ from the reference program's by a relative error of at most 0.015.
Values may be sent and summed in bfloat16 or wider, within the bound.
No kernel may reach another device: no remote copies, remote signals or barrier semaphores. Data moves between devices by JAX's collectives and lax.ppermute only.
A program may use at most 128 MiB of HBM per device.

```python
import math
import jax
import jax.numpy as jnp
from jax import lax

D = 2048
HK = 16
HV = 32
DK = 128
DV = 128
FFE = 512
CONV = 4
TOPK = 2
TOK_DEV = 1024
WINDOW_TOKENS = 16384
ROWS = 64
EXPERTS = 16
CAP = 16


def draw_tokens(key, part):
    random_keys = jax.random.split(jax.random.fold_in(key, 3), 3)
    base = jax.random.truncated_normal(random_keys[0], -4.0, 4.0, (WINDOW_TOKENS, D), jnp.float32)
    row_scale = jnp.exp(jax.random.uniform(random_keys[1], (WINDOW_TOKENS, 1), jnp.float32, math.log(0.3), math.log(3.0)))
    col_scale = jnp.exp(jax.random.uniform(random_keys[2], (1, D), jnp.float32, math.log(0.3), math.log(3.0)))
    return (base * row_scale * col_scale).astype(jnp.bfloat16)


def draw_log_decay(key, part):
    random_keys = jax.random.split(jax.random.fold_in(key, 9), 5)
    cutoff = 5
    fast_head = jax.random.randint(random_keys[0], (1, HV), 0, 10) < cutoff
    baseline_rate = jnp.where(fast_head, 1.0 / 40.0, 0.25 / WINDOW_TOKENS)
    segment_spans = jnp.exp2(jax.random.uniform(random_keys[1], (WINDOW_TOKENS // 32, 1, HV), jnp.float32, -1.0, 1.0))
    segment_spans = jnp.broadcast_to(segment_spans, (WINDOW_TOKENS // 32, 32, HV)).reshape(WINDOW_TOKENS, HV)
    coarse_estimate = jax.random.uniform(random_keys[2], (WINDOW_TOKENS, HV), jnp.float32, 0.5, 1.5)
    spike_position = jax.random.randint(random_keys[3], (3,), 0, WINDOW_TOKENS)
    dropped_tokens = jax.random.uniform(random_keys[4], (3, HV), jnp.float32, 0.2, 0.4)
    boundary_marks = (jnp.arange(WINDOW_TOKENS)[:, None] == spike_position[None, :]).astype(jnp.float32)
    spike_amount = jnp.sum(boundary_marks[:, :, None] * (-jnp.log(1.0 - dropped_tokens))[None, :, :], 1)
    return -(baseline_rate * segment_spans * coarse_estimate + spike_amount)


def draw_write_rate(key, part):
    random_keys = jax.random.split(jax.random.fold_in(key, 13), 4)
    cutoff = 5
    strong_head = jax.random.randint(random_keys[0], (1, HV), 0, 10) < cutoff
    head_rate = jnp.exp(jax.random.uniform(random_keys[1], (1, HV), jnp.float32, math.log(0.3), math.log(0.9)))
    coarse_estimate = jax.random.uniform(random_keys[2], (WINDOW_TOKENS, HV), jnp.float32, 0.7, 1.1)
    slow_rate = jnp.exp(jax.random.uniform(random_keys[3], (WINDOW_TOKENS, HV), jnp.float32, math.log(0.15 * DK / WINDOW_TOKENS), math.log(1.5 * DK / WINDOW_TOKENS)))
    return jnp.where(strong_head, head_rate * coarse_estimate, slow_rate)


def draw_expert_ids(key, part):
    random_keys = jax.random.split(jax.random.fold_in(key, 5), 5)
    blocks = WINDOW_TOKENS // ROWS
    groups = WINDOW_TOKENS // TOK_DEV
    hot_group = jax.random.randint(random_keys[0], (groups,), 0, EXPERTS)
    hot_block = jnp.repeat(hot_group, TOK_DEV // ROWS)
    scores = jax.random.randint(random_keys[1], (blocks, ROWS), 0, 65536) * ROWS + jnp.arange(ROWS)[None, :]
    row_order = jnp.argsort(scores, axis=1)
    row_rank = jnp.argsort(row_order, axis=1)
    other_scores = jax.random.randint(random_keys[2], (blocks, EXPERTS - 1), 0, 65536) * EXPERTS + jnp.arange(EXPERTS - 1)[None, :]
    others = jnp.argsort(other_scores, axis=1)
    others = others + (others >= hot_block[:, None]).astype(others.dtype)
    offset = jax.random.randint(random_keys[3], (blocks, 1, 1), 0, EXPERTS - 1)
    slot_k = jnp.arange(TOPK)[None, None, :]
    rank3 = row_rank[:, :, None]
    hot_row = rank3 < CAP
    position = jnp.where(hot_row, rank3 * (TOPK - 1) + slot_k - 1, CAP * (TOPK - 1) + (rank3 - CAP) * TOPK + slot_k)
    position = (position + offset) % (EXPERTS - 1)
    chosen = jnp.take_along_axis(others, position.reshape(blocks, ROWS * TOPK), axis=1).reshape(blocks, ROWS, TOPK)
    canon = jnp.where(hot_row & (slot_k == 0), hot_block[:, None, None], chosen)
    turn = jax.random.randint(random_keys[4], (blocks, ROWS, 1), 0, TOPK)
    rolled = jnp.take_along_axis(canon, (slot_k + turn) % TOPK, axis=2)
    return rolled.reshape(WINDOW_TOKENS, TOPK).astype(jnp.int32)


def level_of(stream_key, extent, cuts, smallest, largest):
    factor_of = 1.0
    for dim, parts in cuts:
        heights = jax.random.uniform(jax.random.fold_in(jax.random.fold_in(stream_key, 6), dim), (parts,), jnp.float32, smallest / len(cuts), largest / len(cuts))
        factor_of = factor_of * jnp.repeat(jnp.exp(heights), extent[dim] // parts).reshape((-1,) + (1,) * (len(extent) - 1 - dim))
    return factor_of


def bell_draw(key, dims, deviation, limit, cuts=(), kind=jnp.bfloat16):
    level = level_of(key, dims, cuts, -0.22, 0.18) if cuts else 1.0
    values = jax.random.normal(key, dims, jnp.float32) * deviation * level
    return jnp.minimum(jnp.maximum(values, -limit), limit).astype(kind)


def setup_inputs(seed: int = 0) -> dict:
    streams_of = jax.random.split(jax.random.key(seed), 20)
    tokens = draw_tokens(jax.random.fold_in(streams_of[19], 71), 0)
    in_gain = jnp.clip(1.0 + 0.18 * jax.random.normal(streams_of[1], (D,), jnp.float32), 0.1, 1.9)
    w_query = bell_draw(streams_of[2], (D, HK * DK), D ** -0.5, 0.125, ((1, 16),))
    w_key = bell_draw(streams_of[3], (D, HK * DK), D ** -0.5, 0.125, ((1, 16),))
    w_value = bell_draw(streams_of[4], (D, HV * DV), D ** -0.5, 0.125, ((1, 16),))
    w_zgate = bell_draw(streams_of[5], (D, HV * DV), D ** -0.5, 0.125, ((1, 16),))
    conv_query = bell_draw(streams_of[6], (CONV, HK * DK), 0.5, 3.0, ((1, 16),), jnp.float32)
    conv_key = bell_draw(streams_of[7], (CONV, HK * DK), 0.5, 3.0, ((1, 16),), jnp.float32)
    conv_value = bell_draw(streams_of[8], (CONV, HV * DV), 0.5, 3.0, ((1, 16),), jnp.float32)
    log_decay = draw_log_decay(jax.random.fold_in(streams_of[19], 71), 0)
    write_rate = draw_write_rate(jax.random.fold_in(streams_of[19], 71), 0)
    norm_gain = jnp.clip(1.0 + 0.18 * jax.random.normal(streams_of[11], (DV,), jnp.float32), 0.1, 1.9)
    w_out = bell_draw(streams_of[12], (HV * DV, D), (HV * DV) ** -0.5, 0.09375, ((0, 16),))
    post_gain = jnp.clip(1.0 + 0.18 * jax.random.normal(streams_of[13], (D,), jnp.float32), 0.1, 1.9)
    expert_ids = draw_expert_ids(jax.random.fold_in(streams_of[19], 71), 0)
    route_weight = jnp.clip(jnp.exp(math.log(1.0) - 2.3025851 * jax.random.uniform(streams_of[15], (WINDOW_TOKENS, TOPK), jnp.float32) ** level_of(streams_of[15], (WINDOW_TOKENS, TOPK), ((0, 256),), -0.2, 0.2)), 0.1, 1.0)
    w_gate = bell_draw(streams_of[16], (EXPERTS, D, FFE), D ** -0.5, 0.125, ((0, 16),))
    w_up = bell_draw(streams_of[17], (EXPERTS, D, FFE), D ** -0.5, 0.125, ((0, 16),))
    w_down = bell_draw(streams_of[18], (EXPERTS, FFE, D), FFE ** -0.5, 0.25, ((0, 16),))
    return dict(tokens=tokens, in_gain=in_gain, w_query=w_query, w_key=w_key, w_value=w_value, w_zgate=w_zgate, conv_query=conv_query, conv_key=conv_key, conv_value=conv_value, log_decay=log_decay, write_rate=write_rate, norm_gain=norm_gain, w_out=w_out, post_gain=post_gain, expert_ids=expert_ids, route_weight=route_weight, w_gate=w_gate, w_up=w_up, w_down=w_down)


EPS = 1e-06
HIGH = lax.Precision.HIGHEST

def rms_scale(values, gain):
    return values * lax.rsqrt(lax.optimization_barrier(jnp.mean(values * values, -1, keepdims=True)) + EPS) * gain

def short_conv(raw, weights):
    taps = weights.shape[0]
    length = raw.shape[0]
    padded = jnp.concatenate([jnp.zeros((taps - 1, raw.shape[1]), jnp.float32), raw.astype(jnp.float32)], 0)
    mixed = weights[0] * padded[0:length]
    for index in range(1, taps):
        mixed = mixed + weights[index] * padded[index:index + length]
    return jax.nn.silu(mixed)

def unit_heads(values, heads):
    shaped = values.reshape(values.shape[0], heads, -1)
    return shaped * lax.rsqrt(lax.optimization_barrier(jnp.sum(shaped * shaped, -1, keepdims=True)) + EPS)

def reference(tokens, in_gain, w_query, w_key, w_value, w_zgate, conv_query, conv_key, conv_value, log_decay, write_rate, norm_gain, w_out, post_gain, expert_ids, route_weight, w_gate, w_up, w_down):
    x_float = tokens.astype(jnp.float32)
    normed = rms_scale(x_float, in_gain).astype(jnp.bfloat16)

    def project(weight):
        return jnp.dot(normed, weight, preferred_element_type=jnp.float32).astype(jnp.bfloat16)
    q_raw = project(w_query)
    k_raw = project(w_key)
    v_raw = project(w_value)
    z_gate = project(w_zgate)
    query = unit_heads(short_conv(q_raw, conv_query), HK) * DK ** (-0.5)
    keyvec = unit_heads(short_conv(k_raw, conv_key), HK)
    values = short_conv(v_raw, conv_value).reshape(WINDOW_TOKENS, HV, DV)
    group = HV // HK
    query = jnp.repeat(query, group, axis=1)
    keyvec = jnp.repeat(keyvec, group, axis=1)

    def advance(state, inputs):
        q_now, k_now, v_now, g_now, b_now = inputs
        decayed = jnp.exp(g_now)[:, None, None] * state
        predicted = jnp.einsum('hvk,hk->hv', decayed, k_now, precision=HIGH)
        update = b_now[:, None] * (v_now - predicted)
        state = decayed + update[:, :, None] * k_now[:, None, :]
        return (state, jnp.einsum('hvk,hk->hv', state, q_now, precision=HIGH))
    start_state = jnp.zeros((HV, DV, DK), jnp.float32)
    _, delta_out = lax.scan(advance, start_state, (query, keyvec, values, log_decay, write_rate))
    gate_z = z_gate.astype(jnp.float32).reshape(WINDOW_TOKENS, HV, DV)
    gated = (rms_scale(delta_out, norm_gain) * jax.nn.silu(gate_z)).astype(jnp.bfloat16).reshape(WINDOW_TOKENS, HV * DV)
    resid = x_float + jnp.dot(gated, w_out, preferred_element_type=jnp.float32)
    post = rms_scale(resid, post_gain).astype(jnp.bfloat16)
    most = min(WINDOW_TOKENS, WINDOW_TOKENS // ROWS * CAP)

    def expert_pass(total, inputs):
        gate_w, up_w, down_w, number = inputs
        named = (expert_ids == number).astype(jnp.int32)
        weight_e = lax.optimization_barrier(jnp.sum(named.astype(jnp.float32) * route_weight, 1))
        picked = jnp.argsort(1 - lax.optimization_barrier(jnp.max(named, 1)), stable=True)[:most].astype(jnp.int32)
        rows_in = post[picked]
        gate_v = jnp.dot(rows_in, gate_w, preferred_element_type=jnp.float32)
        up_v = jnp.dot(rows_in, up_w, preferred_element_type=jnp.float32)
        act = (jax.nn.silu(gate_v) * up_v).astype(jnp.bfloat16)
        result = jnp.dot(act, down_w, preferred_element_type=jnp.float32).astype(jnp.bfloat16)
        total = total.at[picked].add(weight_e[picked][:, None] * result.astype(jnp.float32))
        return (total, None)
    numbers = jnp.arange(EXPERTS).astype(jnp.int32)
    moe_sum, _ = lax.scan(expert_pass, jnp.zeros((WINDOW_TOKENS, D), jnp.float32), (w_gate, w_up, w_down, numbers))
    return (resid + moe_sum).astype(jnp.bfloat16)
```

```python
import jax
import jax.numpy as jnp
from jax import lax
from jax.sharding import Mesh, PartitionSpec as P

DK = 128
DV = 128
STRETCH = 64
EXP = ("z", "core")


EPS = 1e-06
HIGH = lax.Precision.HIGHEST


def passed_along(block, axis, distance):
    devices = range(lax.axis_size(axis))
    route = [(i - distance, i) for i in devices if i - distance in devices]
    return lax.ppermute(block, axis, route)


def exp_index():
    return lax.axis_index("z") * lax.axis_size("core") + lax.axis_index("core")


def rms_scale(values, gain):
    return values * lax.rsqrt(jnp.mean(values * values, -1, keepdims=True) + EPS) * gain


def mix(form, left_arr, right_arr):
    return jnp.einsum(form, left_arr, right_arr, precision=HIGH)


def unit_heads(values, heads):
    shaped = values.reshape(values.shape[0], heads, -1)
    return shaped * lax.rsqrt(jnp.sum(shaped * shaped, -1, keepdims=True) + EPS)


def unit_lower_inverse(strict):
    size = strict.shape[-1]
    rows = lax.broadcasted_iota(jnp.int32, (size, size), 0)
    cols = lax.broadcasted_iota(jnp.int32, (size, size), 1)
    inverse = jnp.broadcast_to(jnp.eye(size, dtype=strict.dtype), strict.shape)
    span = 1
    while span < size:
        pick = (
            (rows // (2 * span) == cols // (2 * span))
            & ((rows // span) % 2 == 1)
            & ((cols // span) % 2 == 0)
        )
        coupling = jnp.where(pick, strict, 0.0)
        spread = lax.optimization_barrier(mix("...ij,...jk->...ik", coupling, inverse))
        inverse = inverse - lax.optimization_barrier(mix("...ij,...jk->...ik", inverse, spread))
        span *= 2
    return inverse


def compose(first_map, first_add, then_map, then_add):
    stacked = jnp.concatenate([first_map, first_add], -2)
    moved = mix("...kl,...lm->...km", stacked, then_map)
    rows = first_map.shape[-2]
    return moved[..., :rows, :], moved[..., rows:, :] + then_add


def block_prefix(maps, adds):
    count = maps.shape[1]
    eye = jnp.eye(maps.shape[-1], dtype=maps.dtype)
    shift = 1
    while shift < count:
        pad_map = jnp.broadcast_to(eye, maps[:, :shift].shape)
        pad_add = jnp.zeros_like(adds[:, :shift])
        prev_map = jnp.concatenate([pad_map, maps[:, :-shift]], 1)
        prev_add = jnp.concatenate([pad_add, adds[:, :-shift]], 1)
        maps, adds = compose(prev_map, prev_add, maps, adds)
        shift *= 2
    return maps, adds


def shard_prefix(total_map, total_add):
    place = lax.axis_index("seq")
    count = lax.axis_size("seq")
    maps, adds = total_map, total_add
    shift = 1
    while shift < count:
        got = passed_along(jnp.stack([maps, adds]), "seq", shift)
        new_map, new_add = compose(got[0], got[1], maps, adds)
        later = place >= shift
        maps = jnp.where(later, new_map, maps)
        adds = jnp.where(later, new_add, adds)
        shift *= 2
    return passed_along(adds, "seq", 1)


def per_device(
    tokens,
    in_gain,
    w_query,
    w_key,
    w_value,
    w_zgate,
    conv_query,
    conv_key,
    conv_value,
    log_decay,
    write_rate,
    norm_gain,
    w_out,
    post_gain,
    expert_ids,
    route_weight,
    w_gate,
    w_up,
    w_down,
):
    near = lax.all_gather(tokens, "z", axis=0)
    both = lax.all_gather(near, "core", axis=0)
    whole = both.transpose(2, 1, 0, 3).reshape(tokens.shape[0], -1)
    x_float = whole.astype(jnp.float32)
    normed = rms_scale(x_float, in_gain).astype(jnp.bfloat16)

    def project(weight):
        return jnp.dot(normed, weight, preferred_element_type=jnp.float32).astype(jnp.bfloat16)

    projected = jnp.concatenate([project(w_query), project(w_key), project(w_value)], 1)
    z_gate = project(w_zgate)
    conv_all = jnp.concatenate([conv_query, conv_key, conv_value], 1)
    taps = conv_all.shape[0]
    length = projected.shape[0]
    tail = projected[length - (taps - 1) :]
    before = passed_along(tail, "seq", 1)
    extended = jnp.concatenate([before, projected], 0).astype(jnp.float32)
    conv_out = conv_all[0] * extended[0:length]
    for index in range(1, taps):
        conv_out = conv_out + conv_all[index] * extended[index : index + length]
    conv_out = jax.nn.silu(conv_out)
    width_q = w_query.shape[1]
    width_k = w_key.shape[1]
    key_heads = width_q // DK
    value_heads = w_value.shape[1] // DV
    group = value_heads // key_heads
    query = unit_heads(conv_out[:, :width_q], key_heads) * DK ** (-0.5)
    keyvec = unit_heads(conv_out[:, width_q : width_q + width_k], key_heads)
    values = conv_out[:, width_q + width_k :].reshape(length, value_heads, DV)
    query = jnp.repeat(query, group, axis=1)
    keyvec = jnp.repeat(keyvec, group, axis=1)
    blocks = length // STRETCH

    def by_block(array):
        return array.reshape(blocks, STRETCH, value_heads, -1).transpose(2, 0, 1, 3)

    q_blk = by_block(query)
    k_blk = by_block(keyvec)
    v_blk = by_block(values)
    g_blk = log_decay.reshape(blocks, STRETCH, value_heads).transpose(2, 0, 1)
    b_blk = write_rate.reshape(blocks, STRETCH, value_heads).transpose(2, 0, 1)
    cumul = jnp.cumsum(g_blk, -1)
    last_cum = cumul[..., -1:]
    places = jnp.arange(STRETCH)
    lower_incl = places[:, None] >= places[None, :]
    lower_strict = places[:, None] > places[None, :]
    spread_log = cumul[..., :, None] - cumul[..., None, :]
    ratio_incl = jnp.where(lower_incl, jnp.exp(jnp.where(lower_incl, spread_log, 0.0)), 0.0)
    key_gram = mix("hnid,hnjd->hnij", k_blk, k_blk)
    strict = jnp.where(lower_strict, b_blk[..., None] * key_gram * ratio_incl, 0.0)
    inverse = unit_lower_inverse(strict)
    decay_in = jnp.exp(cumul)[..., None]
    right_side = jnp.concatenate(
        [b_blk[..., None] * decay_in * k_blk, b_blk[..., None] * v_blk], -1
    )
    solved = mix("hnij,hnjc->hnic", inverse, right_side)
    w_mat = solved[..., :DK]
    u_mat = solved[..., DK:]
    key_tail = k_blk * jnp.exp(last_cum - cumul)[..., None]
    eye_key = jnp.eye(DK, dtype=jnp.float32)
    transit = jnp.exp(last_cum)[..., None] * eye_key - mix("hnik,hnil->hnkl", w_mat, key_tail)
    inject = mix("hniv,hnik->hnvk", u_mat, key_tail)
    map_incl, add_incl = block_prefix(transit, inject)
    ident_maps = jnp.broadcast_to(eye_key, (value_heads, 1, DK, DK))
    zero_add = jnp.zeros((value_heads, 1, DV, DK), jnp.float32)
    map_prefix = jnp.concatenate([ident_maps, map_incl[:, :-1]], 1)
    add_prefix = jnp.concatenate([zero_add, add_incl[:, :-1]], 1)
    incoming = shard_prefix(map_incl[:, -1], add_incl[:, -1])
    starts = mix("hvk,hnkl->hnvl", incoming, map_prefix) + add_prefix
    new_values = u_mat - mix("hnik,hnvk->hniv", w_mat, starts)
    scores = mix("hnid,hnjd->hnij", q_blk, k_blk) * ratio_incl
    out_blk = decay_in * mix("hnik,hnvk->hniv", q_blk, starts) + mix(
        "hnij,hnjv->hniv", scores, new_values
    )
    delta_out = out_blk.transpose(1, 2, 0, 3).reshape(length, value_heads, DV)
    gate_z = z_gate.astype(jnp.float32).reshape(length, value_heads, DV)
    gated = (
        (rms_scale(delta_out, norm_gain) * jax.nn.silu(gate_z))
        .astype(jnp.bfloat16)
        .reshape(length, value_heads * DV)
    )
    n_exp = lax.axis_size("z") * lax.axis_size("core")
    row_share = length // n_exp
    projected_out = jnp.dot(gated, w_out, preferred_element_type=jnp.float32).astype(jnp.bfloat16)
    chips = lax.axis_size("z")
    by_owner = projected_out.reshape(chips, n_exp // chips, row_share, -1)
    chip_sum = lax.psum_scatter(by_owner, "core", scatter_dimension=1, tiled=True)
    attn_rows = lax.psum_scatter(
        chip_sum.reshape(chips, row_share, -1), "z", scatter_dimension=0, tiled=True
    ).reshape(row_share, -1).astype(jnp.float32)
    own_rows = lax.dynamic_slice_in_dim(
        whole, exp_index() * row_share, row_share, 0
    ).astype(jnp.float32)
    resid = own_rows + attn_rows
    post = rms_scale(resid, post_gain).astype(jnp.bfloat16)
    topk = expert_ids.shape[1]
    experts = w_gate.shape[0] * n_exp
    capacity = 2 * row_share * topk // experts
    flat_ids = expert_ids.reshape(-1)
    hits = (flat_ids[:, None] == jnp.arange(experts)[None, :]).astype(jnp.int32)
    earlier_hits = jnp.cumsum(hits, 0) - hits
    slot_of = jnp.sum(earlier_hits * hits, 1)
    target = flat_ids * capacity + slot_of
    route_map = (target[:, None] == jnp.arange(experts * capacity)[None, :]).astype(jnp.bfloat16)
    spread_rows = jnp.repeat(post, topk, axis=0)
    outgoing = jnp.einsum(
        "rp,rd->pd", route_map, spread_rows, preferred_element_type=jnp.float32
    ).astype(jnp.bfloat16)
    outgoing = outgoing.reshape(experts, 1, capacity, post.shape[1])
    batch = lax.all_to_all(outgoing, EXP, split_axis=0, concat_axis=1, tiled=True)
    gate_v = jnp.einsum("esnd,edf->esnf", batch, w_gate, preferred_element_type=jnp.float32)
    up_v = jnp.einsum("esnd,edf->esnf", batch, w_up, preferred_element_type=jnp.float32)
    act = (jax.nn.silu(gate_v) * up_v).astype(jnp.bfloat16)
    processed = jnp.einsum(
        "esnf,efd->esnd", act, w_down, preferred_element_type=jnp.float32
    ).astype(jnp.bfloat16)
    returned = lax.all_to_all(processed, EXP, split_axis=1, concat_axis=0, tiled=True)
    flat_back = returned.reshape(experts * capacity, post.shape[1])
    fetched = jnp.dot(route_map, flat_back, preferred_element_type=jnp.float32).reshape(
        row_share, topk, post.shape[1]
    )
    moe_sum = jnp.sum(route_weight[..., None] * fetched, 1)
    return (resid + moe_sum).astype(jnp.bfloat16)


def solution(mesh):
    grid = mesh.devices.shape
    fine = Mesh(mesh.devices.reshape(grid[0], grid[1] // 2, 2), ("seq", "z", "core"))
    return jax.shard_map(
        per_device,
        mesh=fine,
        in_specs=(
            P("seq", EXP),
            P(),
            P(None, EXP),
            P(None, EXP),
            P(None, EXP),
            P(None, EXP),
            P(None, EXP),
            P(None, EXP),
            P(None, EXP),
            P("seq", EXP),
            P("seq", EXP),
            P(),
            P(EXP, None),
            P(),
            P(("seq", "z", "core"), None),
            P(("seq", "z", "core"), None),
            P(EXP, None, None),
            P(EXP, None, None),
            P(EXP, None, None),
        ),
        out_specs=P(("seq", "z", "core"), None),
        check_vma=False,
    )
```

```python
import jax
import jax.numpy as jnp
from jax import lax
from jax.sharding import PartitionSpec as P

DK = 128
DV = 128
STRETCH = 64
RADIX = 4


EPS = 1e-06
HIGH = lax.Precision.HIGH


def passed_along(block, axis, distance):
    devices = range(lax.axis_size(axis))
    route = [(i - distance, i) for i in devices if i - distance in devices]
    return lax.ppermute(block, axis, route)


def rms_scale(values, gain):
    return values * lax.rsqrt(jnp.mean(values * values, -1, keepdims=True) + EPS) * gain


def mix(form, left_arr, right_arr):
    return jnp.einsum(form, left_arr, right_arr, precision=HIGH)


def unit_heads(values, heads):
    shaped = values.reshape(values.shape[0], heads, -1)
    return shaped * lax.rsqrt(jnp.sum(shaped * shaped, -1, keepdims=True) + EPS)


def unit_lower_inverse(strict):
    size = strict.shape[-1]
    rows = lax.broadcasted_iota(jnp.int32, (size, size), 0)
    cols = lax.broadcasted_iota(jnp.int32, (size, size), 1)
    inverse = jnp.broadcast_to(jnp.eye(size, dtype=strict.dtype), strict.shape)
    span = 1
    while span < size:
        pick = (
            (rows // (2 * span) == cols // (2 * span))
            & ((rows // span) % 2 == 1)
            & ((cols // span) % 2 == 0)
        )
        coupling = jnp.where(pick, strict, 0.0)
        spread = lax.optimization_barrier(mix("...ij,...jk->...ik", coupling, inverse))
        inverse = inverse - lax.optimization_barrier(mix("...ij,...jk->...ik", inverse, spread))
        span *= 2
    return inverse


def compose(first_map, first_add, then_map, then_add):
    stacked = jnp.concatenate([first_map, first_add], -2)
    moved = mix("...kl,...lm->...km", stacked, then_map)
    rows = first_map.shape[-2]
    return moved[..., :rows, :], moved[..., rows:, :] + then_add


def block_prefix(maps, adds):
    count = maps.shape[1]
    eye = jnp.eye(maps.shape[-1], dtype=maps.dtype)
    shift = 1
    while shift < count:
        pad_map = jnp.broadcast_to(eye, maps[:, :shift].shape)
        pad_add = jnp.zeros_like(adds[:, :shift])
        prev_map = jnp.concatenate([pad_map, maps[:, :-shift]], 1)
        prev_add = jnp.concatenate([pad_add, adds[:, :-shift]], 1)
        maps, adds = compose(prev_map, prev_add, maps, adds)
        shift *= 2
    return maps, adds


def shard_prefix(total_map, total_add):
    place = lax.axis_index("seq")
    count = lax.axis_size("seq")
    eye = jnp.broadcast_to(jnp.eye(total_map.shape[-1], dtype=total_map.dtype), total_map.shape)

    def fetch(maps, adds, shift):
        got = passed_along(jnp.stack([maps, adds]), "seq", shift)
        valid = place >= shift
        return jnp.where(valid, got[0], eye), jnp.where(valid, got[1], 0.0)

    maps, adds = total_map, total_add
    window = 1
    while window * RADIX < count:
        parts = [fetch(maps, adds, window * step) for step in range(RADIX - 1, 0, -1)]
        for prev_map, prev_add in parts[1:] + [(maps, adds)]:
            parts[0] = compose(parts[0][0], parts[0][1], prev_map, prev_add)
        maps, adds = parts[0]
        window *= RADIX
    shifts = list(range(1, count, window))[::-1]
    parts = [fetch(maps, adds, shift) for shift in shifts]
    run_map, run_add = parts[0]
    for prev_map, prev_add in parts[1:]:
        run_map, run_add = compose(run_map, run_add, prev_map, prev_add)
    return run_add


def per_device(
    tokens,
    in_gain,
    w_query,
    w_key,
    w_value,
    w_zgate,
    conv_query,
    conv_key,
    conv_value,
    log_decay,
    write_rate,
    norm_gain,
    w_out,
    post_gain,
    expert_ids,
    route_weight,
    w_gate,
    w_up,
    w_down,
):
    whole = lax.all_gather(tokens, "exp", axis=1, tiled=True)
    x_float = whole.astype(jnp.float32)
    normed = rms_scale(x_float, in_gain).astype(jnp.bfloat16)

    def project(weight):
        return jnp.dot(normed, weight, preferred_element_type=jnp.float32).astype(jnp.bfloat16)

    projected = jnp.concatenate([project(w_query), project(w_key), project(w_value)], 1)
    z_gate = project(w_zgate)
    conv_all = jnp.concatenate([conv_query, conv_key, conv_value], 1)
    taps = conv_all.shape[0]
    length = projected.shape[0]
    tail = projected[length - (taps - 1) :]
    before = passed_along(tail, "seq", 1)
    extended = jnp.concatenate([before, projected], 0).astype(jnp.float32)
    conv_out = conv_all[0] * extended[0:length]
    for index in range(1, taps):
        conv_out = conv_out + conv_all[index] * extended[index : index + length]
    conv_out = jax.nn.silu(conv_out)
    width_q = w_query.shape[1]
    width_k = w_key.shape[1]
    key_heads = width_q // DK
    value_heads = w_value.shape[1] // DV
    group = value_heads // key_heads
    query = unit_heads(conv_out[:, :width_q], key_heads) * DK ** (-0.5)
    keyvec = unit_heads(conv_out[:, width_q : width_q + width_k], key_heads)
    values = conv_out[:, width_q + width_k :].reshape(length, value_heads, DV)
    query = jnp.repeat(query, group, axis=1)
    keyvec = jnp.repeat(keyvec, group, axis=1)
    blocks = length // STRETCH

    def by_block(array):
        return array.reshape(blocks, STRETCH, value_heads, -1).transpose(2, 0, 1, 3)

    q_blk = by_block(query)
    k_blk = by_block(keyvec)
    v_blk = by_block(values)
    g_blk = log_decay.reshape(blocks, STRETCH, value_heads).transpose(2, 0, 1)
    b_blk = write_rate.reshape(blocks, STRETCH, value_heads).transpose(2, 0, 1)
    cumul = jnp.cumsum(g_blk, -1)
    last_cum = cumul[..., -1:]
    places = jnp.arange(STRETCH)
    lower_incl = places[:, None] >= places[None, :]
    lower_strict = places[:, None] > places[None, :]
    spread_log = cumul[..., :, None] - cumul[..., None, :]
    ratio_incl = jnp.where(lower_incl, jnp.exp(jnp.where(lower_incl, spread_log, 0.0)), 0.0)
    key_gram = mix("hnid,hnjd->hnij", k_blk, k_blk)
    strict = jnp.where(lower_strict, b_blk[..., None] * key_gram * ratio_incl, 0.0)
    inverse = unit_lower_inverse(strict)
    decay_in = jnp.exp(cumul)[..., None]
    right_side = jnp.concatenate(
        [b_blk[..., None] * decay_in * k_blk, b_blk[..., None] * v_blk], -1
    )
    solved = mix("hnij,hnjc->hnic", inverse, right_side)
    w_mat = solved[..., :DK]
    u_mat = solved[..., DK:]
    key_tail = k_blk * jnp.exp(last_cum - cumul)[..., None]
    eye_key = jnp.eye(DK, dtype=jnp.float32)
    transit = jnp.exp(last_cum)[..., None] * eye_key - mix("hnik,hnil->hnkl", w_mat, key_tail)
    inject = mix("hniv,hnik->hnvk", u_mat, key_tail)
    map_incl, add_incl = block_prefix(transit, inject)
    ident_maps = jnp.broadcast_to(eye_key, (value_heads, 1, DK, DK))
    zero_add = jnp.zeros((value_heads, 1, DV, DK), jnp.float32)
    map_prefix = jnp.concatenate([ident_maps, map_incl[:, :-1]], 1)
    add_prefix = jnp.concatenate([zero_add, add_incl[:, :-1]], 1)
    incoming = shard_prefix(map_incl[:, -1], add_incl[:, -1])
    starts = mix("hvk,hnkl->hnvl", incoming, map_prefix) + add_prefix
    new_values = u_mat - mix("hnik,hnvk->hniv", w_mat, starts)
    scores = mix("hnid,hnjd->hnij", q_blk, k_blk) * ratio_incl
    out_blk = decay_in * mix("hnik,hnvk->hniv", q_blk, starts) + mix(
        "hnij,hnjv->hniv", scores, new_values
    )
    delta_out = out_blk.transpose(1, 2, 0, 3).reshape(length, value_heads, DV)
    gate_z = z_gate.astype(jnp.float32).reshape(length, value_heads, DV)
    gated = (
        (rms_scale(delta_out, norm_gain) * jax.nn.silu(gate_z))
        .astype(jnp.bfloat16)
        .reshape(length, value_heads * DV)
    )
    n_exp = lax.axis_size("exp")
    row_share = length // n_exp
    attn_rows = lax.psum_scatter(
        jnp.dot(gated, w_out, preferred_element_type=jnp.float32).astype(jnp.bfloat16),
        "exp",
        scatter_dimension=0,
        tiled=True,
    ).astype(jnp.float32)
    own_rows = lax.dynamic_slice_in_dim(
        whole, lax.axis_index("exp") * row_share, row_share, 0
    ).astype(jnp.float32)
    resid = own_rows + attn_rows
    post = rms_scale(resid, post_gain).astype(jnp.bfloat16)
    topk = expert_ids.shape[1]
    experts = w_gate.shape[0] * n_exp
    capacity = 2 * row_share * topk // experts
    flat_ids = expert_ids.reshape(-1)
    hits = (flat_ids[:, None] == jnp.arange(experts)[None, :]).astype(jnp.int32)
    earlier_hits = jnp.cumsum(hits, 0) - hits
    slot_of = jnp.sum(earlier_hits * hits, 1)
    target = flat_ids * capacity + slot_of
    route_map = (target[:, None] == jnp.arange(experts * capacity)[None, :]).astype(jnp.bfloat16)
    spread_rows = jnp.repeat(post, topk, axis=0)
    outgoing = jnp.einsum(
        "rp,rd->pd", route_map, spread_rows, preferred_element_type=jnp.float32
    ).astype(jnp.bfloat16)
    outgoing = outgoing.reshape(experts, 1, capacity, post.shape[1])
    batch = lax.all_to_all(outgoing, "exp", split_axis=0, concat_axis=1, tiled=True)
    gate_v = jnp.einsum("esnd,edf->esnf", batch, w_gate, preferred_element_type=jnp.float32)
    up_v = jnp.einsum("esnd,edf->esnf", batch, w_up, preferred_element_type=jnp.float32)
    act = (jax.nn.silu(gate_v) * up_v).astype(jnp.bfloat16)
    processed = jnp.einsum(
        "esnf,efd->esnd", act, w_down, preferred_element_type=jnp.float32
    ).astype(jnp.bfloat16)
    returned = lax.all_to_all(processed, "exp", split_axis=1, concat_axis=0, tiled=True)
    flat_back = returned.reshape(experts * capacity, post.shape[1])
    fetched = jnp.dot(route_map, flat_back, preferred_element_type=jnp.float32).reshape(
        row_share, topk, post.shape[1]
    )
    moe_sum = jnp.sum(route_weight[..., None] * fetched, 1)
    return (resid + moe_sum).astype(jnp.bfloat16)


def solution(mesh):
    return jax.shard_map(
        per_device,
        mesh=mesh,
        in_specs=(
            P("seq", "exp"),
            P(),
            P(None, "exp"),
            P(None, "exp"),
            P(None, "exp"),
            P(None, "exp"),
            P(None, "exp"),
            P(None, "exp"),
            P(None, "exp"),
            P("seq", "exp"),
            P("seq", "exp"),
            P(),
            P("exp", None),
            P(),
            P(("seq", "exp"), None),
            P(("seq", "exp"), None),
            P("exp", None, None),
            P("exp", None, None),
            P("exp", None, None),
        ),
        out_specs=P(("seq", "exp"), None),
        check_vma=False,
    )
```

```python
import jax
import jax.numpy as jnp
from jax import lax
from jax.sharding import PartitionSpec as P

DK = 128
DV = 128
STRETCH = 64
RADIX = 4


EPS = 1e-06
HIGH = lax.Precision.HIGH


def passed_along(block, axis, distance):
    devices = range(lax.axis_size(axis))
    route = [(i - distance, i) for i in devices if i - distance in devices]
    return lax.ppermute(block, axis, route)


def rms_scale(values, gain):
    return values * lax.rsqrt(jnp.mean(values * values, -1, keepdims=True) + EPS) * gain


def mix(form, left_arr, right_arr):
    return jnp.einsum(form, left_arr, right_arr, precision=HIGH)


def unit_heads(values, heads):
    shaped = values.reshape(values.shape[0], heads, -1)
    return shaped * lax.rsqrt(jnp.sum(shaped * shaped, -1, keepdims=True) + EPS)


def unit_lower_inverse(strict):
    size = strict.shape[-1]
    rows = lax.broadcasted_iota(jnp.int32, (size, size), 0)
    cols = lax.broadcasted_iota(jnp.int32, (size, size), 1)
    inverse = jnp.broadcast_to(jnp.eye(size, dtype=strict.dtype), strict.shape)
    span = 1
    while span < size:
        pick = (
            (rows // (2 * span) == cols // (2 * span))
            & ((rows // span) % 2 == 1)
            & ((cols // span) % 2 == 0)
        )
        coupling = jnp.where(pick, strict, 0.0)
        spread = lax.optimization_barrier(mix("...ij,...jk->...ik", coupling, inverse))
        inverse = inverse - lax.optimization_barrier(mix("...ij,...jk->...ik", inverse, spread))
        span *= 2
    return inverse


def compose(first_map, first_add, then_map, then_add):
    stacked = jnp.concatenate([first_map, first_add], -2)
    moved = mix("...kl,...lm->...km", stacked, then_map)
    rows = first_map.shape[-2]
    return moved[..., :rows, :], moved[..., rows:, :] + then_add


def block_prefix(maps, adds):
    count = maps.shape[1]
    eye = jnp.eye(maps.shape[-1], dtype=maps.dtype)
    shift = 1
    while shift < count:
        pad_map = jnp.broadcast_to(eye, maps[:, :shift].shape)
        pad_add = jnp.zeros_like(adds[:, :shift])
        prev_map = jnp.concatenate([pad_map, maps[:, :-shift]], 1)
        prev_add = jnp.concatenate([pad_add, adds[:, :-shift]], 1)
        maps, adds = compose(prev_map, prev_add, maps, adds)
        shift *= 2
    return maps, adds


def block_total(maps, adds):
    while maps.shape[1] > 1:
        maps, adds = compose(maps[:, 0::2], adds[:, 0::2], maps[:, 1::2], adds[:, 1::2])
    return maps[:, 0], adds[:, 0]


def shard_prefix(total_map, total_add):
    place = lax.axis_index("seq")
    count = lax.axis_size("seq")
    eye = jnp.broadcast_to(jnp.eye(total_map.shape[-1], dtype=total_map.dtype), total_map.shape)

    def fetch(maps, adds, shift):
        got = passed_along(jnp.stack([maps, adds]), "seq", shift)
        valid = place >= shift
        return jnp.where(valid, got[0], eye), jnp.where(valid, got[1], 0.0)

    maps, adds = total_map, total_add
    window = 1
    while window * RADIX < count:
        parts = [fetch(maps, adds, window * step) for step in range(RADIX - 1, 0, -1)]
        for prev_map, prev_add in parts[1:] + [(maps, adds)]:
            parts[0] = compose(parts[0][0], parts[0][1], prev_map, prev_add)
        maps, adds = parts[0]
        window *= RADIX
    shifts = list(range(1, count, window))[::-1]
    parts = [fetch(maps, adds, shift) for shift in shifts]
    run_map, run_add = parts[0]
    for prev_map, prev_add in parts[1:]:
        run_map, run_add = compose(run_map, run_add, prev_map, prev_add)
    return run_add


def per_device(
    tokens,
    in_gain,
    w_query,
    w_key,
    w_value,
    w_zgate,
    conv_query,
    conv_key,
    conv_value,
    log_decay,
    write_rate,
    norm_gain,
    w_out,
    post_gain,
    expert_ids,
    route_weight,
    w_gate,
    w_up,
    w_down,
):
    whole = lax.all_gather(tokens, "exp", axis=1, tiled=True)
    x_float = whole.astype(jnp.float32)
    normed = rms_scale(x_float, in_gain).astype(jnp.bfloat16)

    def project(rows, weight):
        return jnp.dot(rows, weight, preferred_element_type=jnp.float32).astype(jnp.bfloat16)

    conv_all = jnp.concatenate([conv_query, conv_key, conv_value], 1)
    taps = conv_all.shape[0]
    length = normed.shape[0]
    last_rows = normed[length - (taps - 1) :]
    tail = jnp.concatenate([project(last_rows, w) for w in (w_query, w_key, w_value)], 1)
    before = passed_along(tail, "seq", 1)
    projected = jnp.concatenate([project(normed, w) for w in (w_query, w_key, w_value)], 1)
    z_gate = project(normed, w_zgate)
    extended = jnp.concatenate([before, projected], 0).astype(jnp.float32)
    conv_out = conv_all[0] * extended[0:length]
    for index in range(1, taps):
        conv_out = conv_out + conv_all[index] * extended[index : index + length]
    conv_out = jax.nn.silu(conv_out)
    width_q = w_query.shape[1]
    width_k = w_key.shape[1]
    key_heads = width_q // DK
    value_heads = w_value.shape[1] // DV
    group = value_heads // key_heads
    query = unit_heads(conv_out[:, :width_q], key_heads) * DK ** (-0.5)
    keyvec = unit_heads(conv_out[:, width_q : width_q + width_k], key_heads)
    values = conv_out[:, width_q + width_k :].reshape(length, value_heads, DV)
    query = jnp.repeat(query, group, axis=1)
    keyvec = jnp.repeat(keyvec, group, axis=1)
    blocks = length // STRETCH

    def by_block(array):
        return array.reshape(blocks, STRETCH, value_heads, -1).transpose(2, 0, 1, 3)

    q_blk = by_block(query)
    k_blk = by_block(keyvec)
    v_blk = by_block(values)
    g_blk = log_decay.reshape(blocks, STRETCH, value_heads).transpose(2, 0, 1)
    b_blk = write_rate.reshape(blocks, STRETCH, value_heads).transpose(2, 0, 1)
    cumul = jnp.cumsum(g_blk, -1)
    last_cum = cumul[..., -1:]
    places = jnp.arange(STRETCH)
    lower_incl = places[:, None] >= places[None, :]
    lower_strict = places[:, None] > places[None, :]
    spread_log = cumul[..., :, None] - cumul[..., None, :]
    ratio_incl = jnp.where(lower_incl, jnp.exp(jnp.where(lower_incl, spread_log, 0.0)), 0.0)
    key_gram = mix("hnid,hnjd->hnij", k_blk, k_blk)
    strict = jnp.where(lower_strict, b_blk[..., None] * key_gram * ratio_incl, 0.0)
    inverse = unit_lower_inverse(strict)
    decay_in = jnp.exp(cumul)[..., None]
    right_side = jnp.concatenate(
        [b_blk[..., None] * decay_in * k_blk, b_blk[..., None] * v_blk], -1
    )
    solved = mix("hnij,hnjc->hnic", inverse, right_side)
    w_mat = solved[..., :DK]
    u_mat = solved[..., DK:]
    key_tail = k_blk * jnp.exp(last_cum - cumul)[..., None]
    eye_key = jnp.eye(DK, dtype=jnp.float32)
    transit = jnp.exp(last_cum)[..., None] * eye_key - mix("hnik,hnil->hnkl", w_mat, key_tail)
    inject = mix("hniv,hnik->hnvk", u_mat, key_tail)
    total_map, total_add = block_total(transit, inject)
    incoming = shard_prefix(total_map, total_add)
    map_incl, add_incl = block_prefix(transit, inject)
    ident_maps = jnp.broadcast_to(eye_key, (value_heads, 1, DK, DK))
    zero_add = jnp.zeros((value_heads, 1, DV, DK), jnp.float32)
    map_prefix = jnp.concatenate([ident_maps, map_incl[:, :-1]], 1)
    add_prefix = jnp.concatenate([zero_add, add_incl[:, :-1]], 1)
    scores = mix("hnid,hnjd->hnij", q_blk, k_blk) * ratio_incl
    reach = decay_in * q_blk - mix("hnij,hnjk->hnik", scores, w_mat)
    carried = mix("hnik,hnlk->hnil", reach, map_prefix)
    local = mix("hnik,hnvk->hniv", reach, add_prefix) + mix("hnij,hnjv->hniv", scores, u_mat)
    out_blk = mix("hnil,hvl->hniv", carried, incoming) + local
    delta_out = out_blk.transpose(1, 2, 0, 3).reshape(length, value_heads, DV)
    gate_z = z_gate.astype(jnp.float32).reshape(length, value_heads, DV)
    gated = (
        (rms_scale(delta_out, norm_gain) * jax.nn.silu(gate_z))
        .astype(jnp.bfloat16)
        .reshape(length, value_heads * DV)
    )
    n_exp = lax.axis_size("exp")
    row_share = length // n_exp
    gated = lax.optimization_barrier(gated)
    attn_rows = lax.psum_scatter(
        jnp.dot(gated, w_out, preferred_element_type=jnp.float32).astype(jnp.bfloat16),
        "exp",
        scatter_dimension=0,
        tiled=True,
    ).astype(jnp.float32)
    own_rows = lax.dynamic_slice_in_dim(
        whole, lax.axis_index("exp") * row_share, row_share, 0
    ).astype(jnp.float32)
    resid = own_rows + attn_rows
    post = rms_scale(resid, post_gain).astype(jnp.bfloat16)
    topk = expert_ids.shape[1]
    experts = w_gate.shape[0] * n_exp
    capacity = 2 * row_share * topk // experts
    flat_ids = expert_ids.reshape(-1)
    hits = (flat_ids[:, None] == jnp.arange(experts)[None, :]).astype(jnp.int32)
    earlier_hits = jnp.cumsum(hits, 0) - hits
    slot_of = jnp.sum(earlier_hits * hits, 1)
    target = flat_ids * capacity + slot_of
    route_map = (target[:, None] == jnp.arange(experts * capacity)[None, :]).astype(jnp.bfloat16)
    spread_rows = jnp.repeat(post, topk, axis=0)
    outgoing = jnp.einsum(
        "rp,rd->pd", route_map, spread_rows, preferred_element_type=jnp.float32
    ).astype(jnp.bfloat16)
    outgoing = outgoing.reshape(experts, 1, capacity, post.shape[1])
    batch = lax.all_to_all(outgoing, "exp", split_axis=0, concat_axis=1, tiled=True)
    gate_v = jnp.einsum("esnd,edf->esnf", batch, w_gate, preferred_element_type=jnp.float32)
    up_v = jnp.einsum("esnd,edf->esnf", batch, w_up, preferred_element_type=jnp.float32)
    act = (jax.nn.silu(gate_v) * up_v).astype(jnp.bfloat16)
    processed = jnp.einsum(
        "esnf,efd->esnd", act, w_down, preferred_element_type=jnp.float32
    ).astype(jnp.bfloat16)
    returned = lax.all_to_all(processed, "exp", split_axis=1, concat_axis=0, tiled=True)
    flat_back = returned.reshape(experts * capacity, post.shape[1])
    fetched = jnp.dot(route_map, flat_back, preferred_element_type=jnp.float32).reshape(
        row_share, topk, post.shape[1]
    )
    moe_sum = jnp.sum(route_weight[..., None] * fetched, 1)
    return (resid + moe_sum).astype(jnp.bfloat16)


def solution(mesh):
    return jax.shard_map(
        per_device,
        mesh=mesh,
        in_specs=(
            P("seq", "exp"),
            P(),
            P(None, "exp"),
            P(None, "exp"),
            P(None, "exp"),
            P(None, "exp"),
            P(None, "exp"),
            P(None, "exp"),
            P(None, "exp"),
            P("seq", "exp"),
            P("seq", "exp"),
            P(),
            P("exp", None),
            P(),
            P(("seq", "exp"), None),
            P(("seq", "exp"), None),
            P("exp", None, None),
            P("exp", None, None),
            P("exp", None, None),
        ),
        out_specs=P(("seq", "exp"), None),
        check_vma=False,
    )
```

```python
import jax
import jax.numpy as jnp
from jax import lax
from jax.sharding import PartitionSpec as P

DK = 128
DV = 128
STRETCH = 64
RADIX = 4


EPS = 1e-06
HIGH = lax.Precision.HIGH


def passed_along(block, axis, distance):
    devices = range(lax.axis_size(axis))
    route = [(i - distance, i) for i in devices if i - distance in devices]
    return lax.ppermute(block, axis, route)


def rms_scale(values, gain):
    return values * lax.rsqrt(jnp.mean(values * values, -1, keepdims=True) + EPS) * gain


def mix(form, left_arr, right_arr):
    return jnp.einsum(form, left_arr, right_arr, precision=HIGH)


def unit_heads(values, heads):
    shaped = values.reshape(values.shape[0], heads, -1)
    return shaped * lax.rsqrt(jnp.sum(shaped * shaped, -1, keepdims=True) + EPS)


def unit_lower_inverse(strict):
    size = strict.shape[-1]
    rows = lax.broadcasted_iota(jnp.int32, (size, size), 0)
    cols = lax.broadcasted_iota(jnp.int32, (size, size), 1)
    inverse = jnp.broadcast_to(jnp.eye(size, dtype=strict.dtype), strict.shape)
    span = 1
    while span < size:
        pick = (
            (rows // (2 * span) == cols // (2 * span))
            & ((rows // span) % 2 == 1)
            & ((cols // span) % 2 == 0)
        )
        coupling = jnp.where(pick, strict, 0.0)
        spread = lax.optimization_barrier(mix("...ij,...jk->...ik", coupling, inverse))
        inverse = inverse - lax.optimization_barrier(mix("...ij,...jk->...ik", inverse, spread))
        span *= 2
    return inverse


def compose(first_map, first_add, then_map, then_add):
    stacked = jnp.concatenate([first_map, first_add], -2)
    moved = mix("...kl,...lm->...km", stacked, then_map)
    rows = first_map.shape[-2]
    return moved[..., :rows, :], moved[..., rows:, :] + then_add


def block_prefix(maps, adds):
    count = maps.shape[1]
    eye = jnp.eye(maps.shape[-1], dtype=maps.dtype)
    shift = 1
    while shift < count:
        pad_map = jnp.broadcast_to(eye, maps[:, :shift].shape)
        pad_add = jnp.zeros_like(adds[:, :shift])
        prev_map = jnp.concatenate([pad_map, maps[:, :-shift]], 1)
        prev_add = jnp.concatenate([pad_add, adds[:, :-shift]], 1)
        maps, adds = compose(prev_map, prev_add, maps, adds)
        shift *= 2
    return maps, adds


def block_total(maps, adds):
    while maps.shape[1] > 1:
        maps, adds = compose(maps[:, 0::2], adds[:, 0::2], maps[:, 1::2], adds[:, 1::2])
    return maps[:, 0], adds[:, 0]


def shard_prefix(total_map, total_add):
    place = lax.axis_index("seq")
    gathered = lax.all_gather(jnp.stack([total_map, total_add]), "seq")
    earlier = (jnp.arange(gathered.shape[0]) < place)[:, None, None, None]
    eye = jnp.eye(total_map.shape[-1], dtype=total_map.dtype)
    maps = jnp.where(earlier, gathered[:, 0], eye)
    adds = jnp.where(earlier, gathered[:, 1], 0.0)
    while maps.shape[0] > 1:
        maps, adds = compose(maps[0::2], adds[0::2], maps[1::2], adds[1::2])
    return adds[0]


def per_device(
    tokens,
    in_gain,
    w_query,
    w_key,
    w_value,
    w_zgate,
    conv_query,
    conv_key,
    conv_value,
    log_decay,
    write_rate,
    norm_gain,
    w_out,
    post_gain,
    expert_ids,
    route_weight,
    w_gate,
    w_up,
    w_down,
):
    whole = lax.all_gather(tokens, "exp", axis=1, tiled=True)
    x_float = whole.astype(jnp.float32)
    normed = rms_scale(x_float, in_gain).astype(jnp.bfloat16)

    def project(rows, weight):
        return jnp.dot(rows, weight, preferred_element_type=jnp.float32).astype(jnp.bfloat16)

    conv_all = jnp.concatenate([conv_query, conv_key, conv_value], 1)
    taps = conv_all.shape[0]
    length = normed.shape[0]
    last_rows = normed[length - (taps - 1) :]
    tail = jnp.concatenate([project(last_rows, w) for w in (w_query, w_key, w_value)], 1)
    before = passed_along(tail, "seq", 1)
    projected = jnp.concatenate([project(normed, w) for w in (w_query, w_key, w_value)], 1)
    z_gate = project(normed, w_zgate)
    extended = jnp.concatenate([before, projected], 0).astype(jnp.float32)
    conv_out = conv_all[0] * extended[0:length]
    for index in range(1, taps):
        conv_out = conv_out + conv_all[index] * extended[index : index + length]
    conv_out = jax.nn.silu(conv_out)
    width_q = w_query.shape[1]
    width_k = w_key.shape[1]
    key_heads = width_q // DK
    value_heads = w_value.shape[1] // DV
    group = value_heads // key_heads
    query = unit_heads(conv_out[:, :width_q], key_heads) * DK ** (-0.5)
    keyvec = unit_heads(conv_out[:, width_q : width_q + width_k], key_heads)
    values = conv_out[:, width_q + width_k :].reshape(length, value_heads, DV)
    query = jnp.repeat(query, group, axis=1)
    keyvec = jnp.repeat(keyvec, group, axis=1)
    blocks = length // STRETCH

    def by_block(array):
        return array.reshape(blocks, STRETCH, value_heads, -1).transpose(2, 0, 1, 3)

    q_blk = by_block(query)
    k_blk = by_block(keyvec)
    v_blk = by_block(values)
    g_blk = log_decay.reshape(blocks, STRETCH, value_heads).transpose(2, 0, 1)
    b_blk = write_rate.reshape(blocks, STRETCH, value_heads).transpose(2, 0, 1)
    cumul = jnp.cumsum(g_blk, -1)
    last_cum = cumul[..., -1:]
    places = jnp.arange(STRETCH)
    lower_incl = places[:, None] >= places[None, :]
    lower_strict = places[:, None] > places[None, :]
    spread_log = cumul[..., :, None] - cumul[..., None, :]
    ratio_incl = jnp.where(lower_incl, jnp.exp(jnp.where(lower_incl, spread_log, 0.0)), 0.0)
    key_gram = mix("hnid,hnjd->hnij", k_blk, k_blk)
    strict = jnp.where(lower_strict, b_blk[..., None] * key_gram * ratio_incl, 0.0)
    inverse = unit_lower_inverse(strict)
    decay_in = jnp.exp(cumul)[..., None]
    right_side = jnp.concatenate(
        [b_blk[..., None] * decay_in * k_blk, b_blk[..., None] * v_blk], -1
    )
    solved = mix("hnij,hnjc->hnic", inverse, right_side)
    w_mat = solved[..., :DK]
    u_mat = solved[..., DK:]
    key_tail = k_blk * jnp.exp(last_cum - cumul)[..., None]
    eye_key = jnp.eye(DK, dtype=jnp.float32)
    transit = jnp.exp(last_cum)[..., None] * eye_key - mix("hnik,hnil->hnkl", w_mat, key_tail)
    inject = mix("hniv,hnik->hnvk", u_mat, key_tail)
    total_map, total_add = block_total(transit, inject)
    incoming = shard_prefix(total_map, total_add)
    map_incl, add_incl = block_prefix(transit, inject)
    ident_maps = jnp.broadcast_to(eye_key, (value_heads, 1, DK, DK))
    zero_add = jnp.zeros((value_heads, 1, DV, DK), jnp.float32)
    map_prefix = jnp.concatenate([ident_maps, map_incl[:, :-1]], 1)
    add_prefix = jnp.concatenate([zero_add, add_incl[:, :-1]], 1)
    scores = mix("hnid,hnjd->hnij", q_blk, k_blk) * ratio_incl
    reach = decay_in * q_blk - mix("hnij,hnjk->hnik", scores, w_mat)
    carried = mix("hnik,hnlk->hnil", reach, map_prefix)
    local = mix("hnik,hnvk->hniv", reach, add_prefix) + mix("hnij,hnjv->hniv", scores, u_mat)
    out_blk = mix("hnil,hvl->hniv", carried, incoming) + local
    delta_out = out_blk.transpose(1, 2, 0, 3).reshape(length, value_heads, DV)
    gate_z = z_gate.astype(jnp.float32).reshape(length, value_heads, DV)
    gated = (
        (rms_scale(delta_out, norm_gain) * jax.nn.silu(gate_z))
        .astype(jnp.bfloat16)
        .reshape(length, value_heads * DV)
    )
    n_exp = lax.axis_size("exp")
    row_share = length // n_exp
    gated = lax.optimization_barrier(gated)
    attn_rows = lax.psum_scatter(
        jnp.dot(gated, w_out, preferred_element_type=jnp.float32).astype(jnp.bfloat16),
        "exp",
        scatter_dimension=0,
        tiled=True,
    ).astype(jnp.float32)
    own_rows = lax.dynamic_slice_in_dim(
        whole, lax.axis_index("exp") * row_share, row_share, 0
    ).astype(jnp.float32)
    resid = own_rows + attn_rows
    post = rms_scale(resid, post_gain).astype(jnp.bfloat16)
    topk = expert_ids.shape[1]
    experts = w_gate.shape[0] * n_exp
    capacity = 2 * row_share * topk // experts
    flat_ids = expert_ids.reshape(-1)
    hits = (flat_ids[:, None] == jnp.arange(experts)[None, :]).astype(jnp.int32)
    earlier_hits = jnp.cumsum(hits, 0) - hits
    slot_of = jnp.sum(earlier_hits * hits, 1)
    target = flat_ids * capacity + slot_of
    route_map = (target[:, None] == jnp.arange(experts * capacity)[None, :]).astype(jnp.bfloat16)
    spread_rows = jnp.repeat(post, topk, axis=0)
    outgoing = jnp.einsum(
        "rp,rd->pd", route_map, spread_rows, preferred_element_type=jnp.float32
    ).astype(jnp.bfloat16)
    outgoing = outgoing.reshape(experts, 1, capacity, post.shape[1])
    batch = lax.all_to_all(outgoing, "exp", split_axis=0, concat_axis=1, tiled=True)
    gate_v = jnp.einsum("esnd,edf->esnf", batch, w_gate, preferred_element_type=jnp.float32)
    up_v = jnp.einsum("esnd,edf->esnf", batch, w_up, preferred_element_type=jnp.float32)
    act = (jax.nn.silu(gate_v) * up_v).astype(jnp.bfloat16)
    processed = jnp.einsum(
        "esnf,efd->esnd", act, w_down, preferred_element_type=jnp.float32
    ).astype(jnp.bfloat16)
    returned = lax.all_to_all(processed, "exp", split_axis=1, concat_axis=0, tiled=True)
    flat_back = returned.reshape(experts * capacity, post.shape[1])
    fetched = jnp.dot(route_map, flat_back, preferred_element_type=jnp.float32).reshape(
        row_share, topk, post.shape[1]
    )
    moe_sum = jnp.sum(route_weight[..., None] * fetched, 1)
    return (resid + moe_sum).astype(jnp.bfloat16)


def solution(mesh):
    return jax.shard_map(
        per_device,
        mesh=mesh,
        in_specs=(
            P("seq", "exp"),
            P(),
            P(None, "exp"),
            P(None, "exp"),
            P(None, "exp"),
            P(None, "exp"),
            P(None, "exp"),
            P(None, "exp"),
            P(None, "exp"),
            P("seq", "exp"),
            P("seq", "exp"),
            P(),
            P("exp", None),
            P(),
            P(("seq", "exp"), None),
            P(("seq", "exp"), None),
            P("exp", None, None),
            P("exp", None, None),
            P("exp", None, None),
        ),
        out_specs=P(("seq", "exp"), None),
        check_vma=False,
    )
```

```python
import jax
import jax.numpy as jnp
from jax import lax
from jax.sharding import PartitionSpec as P

DK = 128
DV = 128
STRETCH = 64
RADIX = 4


EPS = 1e-06
HIGH = lax.Precision.HIGH


def passed_along(block, axis, distance):
    devices = range(lax.axis_size(axis))
    route = [(i - distance, i) for i in devices if i - distance in devices]
    return lax.ppermute(block, axis, route)


def rms_scale(values, gain):
    return values * lax.rsqrt(jnp.mean(values * values, -1, keepdims=True) + EPS) * gain


def mix(form, left_arr, right_arr):
    return jnp.einsum(form, left_arr, right_arr, precision=HIGH)


def unit_heads(values, heads):
    shaped = values.reshape(values.shape[0], heads, -1)
    return shaped * lax.rsqrt(jnp.sum(shaped * shaped, -1, keepdims=True) + EPS)


def unit_lower_inverse(strict):
    size = strict.shape[-1]
    rows = lax.broadcasted_iota(jnp.int32, (size, size), 0)
    cols = lax.broadcasted_iota(jnp.int32, (size, size), 1)
    inverse = jnp.broadcast_to(jnp.eye(size, dtype=strict.dtype), strict.shape)
    span = 1
    while span < size:
        pick = (
            (rows // (2 * span) == cols // (2 * span))
            & ((rows // span) % 2 == 1)
            & ((cols // span) % 2 == 0)
        )
        coupling = jnp.where(pick, strict, 0.0)
        spread = lax.optimization_barrier(mix("...ij,...jk->...ik", coupling, inverse))
        inverse = inverse - lax.optimization_barrier(mix("...ij,...jk->...ik", inverse, spread))
        span *= 2
    return inverse


def compose(first_map, first_add, then_map, then_add):
    stacked = jnp.concatenate([first_map, first_add], -2)
    moved = mix("...kl,...lm->...km", stacked, then_map)
    rows = first_map.shape[-2]
    return moved[..., :rows, :], moved[..., rows:, :] + then_add


def block_prefix(maps, adds):
    count = maps.shape[1]
    eye = jnp.eye(maps.shape[-1], dtype=maps.dtype)
    shift = 1
    while shift < count:
        pad_map = jnp.broadcast_to(eye, maps[:, :shift].shape)
        pad_add = jnp.zeros_like(adds[:, :shift])
        prev_map = jnp.concatenate([pad_map, maps[:, :-shift]], 1)
        prev_add = jnp.concatenate([pad_add, adds[:, :-shift]], 1)
        maps, adds = compose(prev_map, prev_add, maps, adds)
        shift *= 2
    return maps, adds


def block_total(maps, adds):
    while maps.shape[1] > 1:
        maps, adds = compose(maps[:, 0::2], adds[:, 0::2], maps[:, 1::2], adds[:, 1::2])
    return maps[:, 0], adds[:, 0]


def shard_prefix(total_map, total_add):
    place = lax.axis_index("seq")
    gathered = lax.all_gather(jnp.stack([total_map, total_add]), "seq")
    earlier = (jnp.arange(gathered.shape[0]) < place)[:, None, None, None]
    eye = jnp.eye(total_map.shape[-1], dtype=total_map.dtype)
    maps = jnp.where(earlier, gathered[:, 0], eye)
    adds = jnp.where(earlier, gathered[:, 1], 0.0)
    while maps.shape[0] > 1:
        maps, adds = compose(maps[0::2], adds[0::2], maps[1::2], adds[1::2])
    return adds[0]


def per_device(
    tokens,
    in_gain,
    w_query,
    w_key,
    w_value,
    w_zgate,
    conv_query,
    conv_key,
    conv_value,
    log_decay,
    write_rate,
    norm_gain,
    w_out,
    post_gain,
    expert_ids,
    route_weight,
    w_gate,
    w_up,
    w_down,
):
    whole = lax.all_gather(tokens, "exp", axis=1, tiled=True)
    x_float = whole.astype(jnp.float32)
    normed = rms_scale(x_float, in_gain).astype(jnp.bfloat16)

    def project(rows, weight):
        return jnp.dot(rows, weight, preferred_element_type=jnp.float32).astype(jnp.bfloat16)

    value_heads = w_value.shape[1] // DV

    def project_heads(rows, weight):
        split = weight.reshape(weight.shape[0], value_heads, -1)
        return jnp.einsum(
            "td,dhe->hte", rows, split, preferred_element_type=jnp.float32
        ).astype(jnp.bfloat16)

    conv_all = jnp.concatenate([conv_query, conv_key], 1)
    taps = conv_all.shape[0]
    length = normed.shape[0]
    last_rows = normed[length - (taps - 1) :]
    tail_v = project_heads(last_rows, w_value)
    tail = jnp.concatenate(
        [project(last_rows, w) for w in (w_query, w_key)]
        + [tail_v.transpose(1, 0, 2).reshape(taps - 1, -1)],
        1,
    )
    before = passed_along(tail, "seq", 1)
    projected = jnp.concatenate([project(normed, w) for w in (w_query, w_key)], 1)
    v_raw = project_heads(normed, w_value)
    z_heads = project_heads(normed, w_zgate)
    width_q = w_query.shape[1]
    width_k = w_key.shape[1]
    split_at = width_q + width_k
    extended = jnp.concatenate([before[:, :split_at], projected], 0).astype(jnp.float32)
    conv_out = conv_all[0] * extended[0:length]
    for index in range(1, taps):
        conv_out = conv_out + conv_all[index] * extended[index : index + length]
    conv_out = jax.nn.silu(conv_out)
    before_v = before[:, split_at:].reshape(taps - 1, value_heads, DV).transpose(1, 0, 2)
    extended_v = jnp.concatenate([before_v, v_raw], 1).astype(jnp.float32)
    taps_v = conv_value.reshape(taps, value_heads, 1, DV)
    conv_v = taps_v[0] * extended_v[:, 0:length]
    for index in range(1, taps):
        conv_v = conv_v + taps_v[index] * extended_v[:, index : index + length]
    conv_v = jax.nn.silu(conv_v)
    key_heads = width_q // DK
    group = value_heads // key_heads
    query = unit_heads(conv_out[:, :width_q], key_heads) * DK ** (-0.5)
    keyvec = unit_heads(conv_out[:, width_q : width_q + width_k], key_heads)
    query = jnp.repeat(query, group, axis=1)
    keyvec = jnp.repeat(keyvec, group, axis=1)
    blocks = length // STRETCH

    def by_block(array):
        return array.reshape(blocks, STRETCH, value_heads, -1).transpose(2, 0, 1, 3)

    q_blk = by_block(query)
    k_blk = by_block(keyvec)
    v_blk = conv_v.reshape(value_heads, blocks, STRETCH, DV)
    g_blk = log_decay.reshape(blocks, STRETCH, value_heads).transpose(2, 0, 1)
    b_blk = write_rate.reshape(blocks, STRETCH, value_heads).transpose(2, 0, 1)
    cumul = jnp.cumsum(g_blk, -1)
    last_cum = cumul[..., -1:]
    places = jnp.arange(STRETCH)
    lower_incl = places[:, None] >= places[None, :]
    lower_strict = places[:, None] > places[None, :]
    spread_log = cumul[..., :, None] - cumul[..., None, :]
    ratio_incl = jnp.where(lower_incl, jnp.exp(jnp.where(lower_incl, spread_log, 0.0)), 0.0)
    key_gram = mix("hnid,hnjd->hnij", k_blk, k_blk)
    strict = jnp.where(lower_strict, b_blk[..., None] * key_gram * ratio_incl, 0.0)
    inverse = unit_lower_inverse(strict)
    decay_in = jnp.exp(cumul)[..., None]
    right_side = jnp.concatenate(
        [b_blk[..., None] * decay_in * k_blk, b_blk[..., None] * v_blk], -1
    )
    solved = mix("hnij,hnjc->hnic", inverse, right_side)
    w_mat = solved[..., :DK]
    u_mat = solved[..., DK:]
    key_tail = k_blk * jnp.exp(last_cum - cumul)[..., None]
    eye_key = jnp.eye(DK, dtype=jnp.float32)
    transit = jnp.exp(last_cum)[..., None] * eye_key - mix("hnik,hnil->hnkl", w_mat, key_tail)
    inject = mix("hniv,hnik->hnvk", u_mat, key_tail)
    total_map, total_add = block_total(transit, inject)
    incoming = shard_prefix(total_map, total_add)
    map_incl, add_incl = block_prefix(transit, inject)
    ident_maps = jnp.broadcast_to(eye_key, (value_heads, 1, DK, DK))
    zero_add = jnp.zeros((value_heads, 1, DV, DK), jnp.float32)
    map_prefix = jnp.concatenate([ident_maps, map_incl[:, :-1]], 1)
    add_prefix = jnp.concatenate([zero_add, add_incl[:, :-1]], 1)
    scores = mix("hnid,hnjd->hnij", q_blk, k_blk) * ratio_incl
    reach = decay_in * q_blk - mix("hnij,hnjk->hnik", scores, w_mat)
    carried = mix("hnik,hnlk->hnil", reach, map_prefix)
    local = mix("hnik,hnvk->hniv", reach, add_prefix) + mix("hnij,hnjv->hniv", scores, u_mat)
    out_blk = mix("hnil,hvl->hniv", carried, incoming) + local
    delta_out = out_blk.reshape(value_heads, length, DV)
    gate_z = z_heads.astype(jnp.float32)
    gated = (rms_scale(delta_out, norm_gain) * jax.nn.silu(gate_z)).astype(jnp.bfloat16)
    n_exp = lax.axis_size("exp")
    row_share = length // n_exp
    gated = lax.optimization_barrier(gated)
    attn_rows = lax.psum_scatter(
        jnp.einsum(
            "htv,hvd->td",
            gated,
            w_out.reshape(value_heads, DV, -1),
            preferred_element_type=jnp.float32,
        ).astype(jnp.bfloat16),
        "exp",
        scatter_dimension=0,
        tiled=True,
    ).astype(jnp.float32)
    own_rows = lax.dynamic_slice_in_dim(
        whole, lax.axis_index("exp") * row_share, row_share, 0
    ).astype(jnp.float32)
    resid = own_rows + attn_rows
    post = rms_scale(resid, post_gain).astype(jnp.bfloat16)
    topk = expert_ids.shape[1]
    experts = w_gate.shape[0] * n_exp
    capacity = 2 * row_share * topk // experts
    flat_ids = expert_ids.reshape(-1)
    hits = (flat_ids[:, None] == jnp.arange(experts)[None, :]).astype(jnp.int32)
    earlier_hits = jnp.cumsum(hits, 0) - hits
    slot_of = jnp.sum(earlier_hits * hits, 1)
    target = flat_ids * capacity + slot_of
    route_map = (target[:, None] == jnp.arange(experts * capacity)[None, :]).astype(jnp.bfloat16)
    spread_rows = jnp.repeat(post, topk, axis=0)
    outgoing = jnp.einsum(
        "rp,rd->pd", route_map, spread_rows, preferred_element_type=jnp.float32
    ).astype(jnp.bfloat16)
    outgoing = outgoing.reshape(experts, 1, capacity, post.shape[1])
    batch = lax.all_to_all(outgoing, "exp", split_axis=0, concat_axis=1, tiled=True)
    gate_v = jnp.einsum("esnd,edf->esnf", batch, w_gate, preferred_element_type=jnp.float32)
    up_v = jnp.einsum("esnd,edf->esnf", batch, w_up, preferred_element_type=jnp.float32)
    act = (jax.nn.silu(gate_v) * up_v).astype(jnp.bfloat16)
    processed = jnp.einsum(
        "esnf,efd->esnd", act, w_down, preferred_element_type=jnp.float32
    ).astype(jnp.bfloat16)
    returned = lax.all_to_all(processed, "exp", split_axis=1, concat_axis=0, tiled=True)
    flat_back = returned.reshape(experts * capacity, post.shape[1])
    fetched = jnp.dot(route_map, flat_back, preferred_element_type=jnp.float32).reshape(
        row_share, topk, post.shape[1]
    )
    moe_sum = jnp.sum(route_weight[..., None] * fetched, 1)
    return (resid + moe_sum).astype(jnp.bfloat16)


def solution(mesh):
    return jax.shard_map(
        per_device,
        mesh=mesh,
        in_specs=(
            P("seq", "exp"),
            P(),
            P(None, "exp"),
            P(None, "exp"),
            P(None, "exp"),
            P(None, "exp"),
            P(None, "exp"),
            P(None, "exp"),
            P(None, "exp"),
            P("seq", "exp"),
            P("seq", "exp"),
            P(),
            P("exp", None),
            P(),
            P(("seq", "exp"), None),
            P(("seq", "exp"), None),
            P("exp", None, None),
            P("exp", None, None),
            P("exp", None, None),
        ),
        out_specs=P(("seq", "exp"), None),
        check_vma=False,
    )
```

```python
import jax
import jax.numpy as jnp
from jax import lax
from jax.sharding import PartitionSpec as P

DK = 128
DV = 128
STRETCH = 64
RADIX = 4


EPS = 1e-06
HIGH = lax.Precision.HIGH


def passed_along(block, axis, distance):
    devices = range(lax.axis_size(axis))
    route = [(i - distance, i) for i in devices if i - distance in devices]
    return lax.ppermute(block, axis, route)


def rms_scale(values, gain):
    return values * lax.rsqrt(jnp.mean(values * values, -1, keepdims=True) + EPS) * gain


def mix(form, left_arr, right_arr):
    return jnp.einsum(form, left_arr, right_arr, precision=HIGH)


def unit_heads(values, heads):
    shaped = values.reshape(values.shape[0], heads, -1)
    return shaped * lax.rsqrt(jnp.sum(shaped * shaped, -1, keepdims=True) + EPS)


def unit_lower_inverse(strict):
    size = strict.shape[-1]
    rows = lax.broadcasted_iota(jnp.int32, (size, size), 0)
    cols = lax.broadcasted_iota(jnp.int32, (size, size), 1)
    inverse = jnp.broadcast_to(jnp.eye(size, dtype=strict.dtype), strict.shape)
    span = 1
    while span < size:
        pick = (
            (rows // (2 * span) == cols // (2 * span))
            & ((rows // span) % 2 == 1)
            & ((cols // span) % 2 == 0)
        )
        coupling = jnp.where(pick, strict, 0.0)
        spread = lax.optimization_barrier(mix("...ij,...jk->...ik", coupling, inverse))
        inverse = inverse - lax.optimization_barrier(mix("...ij,...jk->...ik", inverse, spread))
        span *= 2
    return inverse


def compose(first_map, first_add, then_map, then_add):
    stacked = jnp.concatenate([first_map, first_add], -2)
    moved = mix("...kl,...lm->...km", stacked, then_map)
    rows = first_map.shape[-2]
    return moved[..., :rows, :], moved[..., rows:, :] + then_add


def block_prefix(maps, adds):
    count = maps.shape[1]
    eye = jnp.eye(maps.shape[-1], dtype=maps.dtype)
    shift = 1
    while shift < count:
        pad_map = jnp.broadcast_to(eye, maps[:, :shift].shape)
        pad_add = jnp.zeros_like(adds[:, :shift])
        prev_map = jnp.concatenate([pad_map, maps[:, :-shift]], 1)
        prev_add = jnp.concatenate([pad_add, adds[:, :-shift]], 1)
        maps, adds = compose(prev_map, prev_add, maps, adds)
        shift *= 2
    return maps, adds


def block_total(maps, adds):
    while maps.shape[1] > 1:
        maps, adds = compose(maps[:, 0::2], adds[:, 0::2], maps[:, 1::2], adds[:, 1::2])
    return maps[:, 0], adds[:, 0]


def shard_prefix(total_map, total_add):
    place = lax.axis_index("seq")
    packed = jnp.stack([total_map, total_add]).astype(jnp.bfloat16)
    gathered = lax.all_gather(packed, "seq").astype(total_map.dtype)
    earlier = (jnp.arange(gathered.shape[0]) < place)[:, None, None, None]
    eye = jnp.eye(total_map.shape[-1], dtype=total_map.dtype)
    maps = jnp.where(earlier, gathered[:, 0], eye)
    adds = jnp.where(earlier, gathered[:, 1], 0.0)
    while maps.shape[0] > 1:
        maps, adds = compose(maps[0::2], adds[0::2], maps[1::2], adds[1::2])
    return adds[0]


def per_device(
    tokens,
    in_gain,
    w_query,
    w_key,
    w_value,
    w_zgate,
    conv_query,
    conv_key,
    conv_value,
    log_decay,
    write_rate,
    norm_gain,
    w_out,
    post_gain,
    expert_ids,
    route_weight,
    w_gate,
    w_up,
    w_down,
):
    whole = lax.all_gather(tokens, "exp", axis=1, tiled=True)
    x_float = whole.astype(jnp.float32)
    normed = rms_scale(x_float, in_gain).astype(jnp.bfloat16)

    def project(rows, weight):
        return jnp.dot(rows, weight, preferred_element_type=jnp.float32).astype(jnp.bfloat16)

    value_heads = w_value.shape[1] // DV

    def project_heads(rows, weight):
        split = weight.reshape(weight.shape[0], value_heads, -1)
        return jnp.einsum(
            "td,dhe->hte", rows, split, preferred_element_type=jnp.float32
        ).astype(jnp.bfloat16)

    conv_all = jnp.concatenate([conv_query, conv_key], 1)
    taps = conv_all.shape[0]
    length = normed.shape[0]
    last_rows = normed[length - (taps - 1) :]
    tail_v = project_heads(last_rows, w_value)
    tail = jnp.concatenate(
        [project(last_rows, w) for w in (w_query, w_key)]
        + [tail_v.transpose(1, 0, 2).reshape(taps - 1, -1)],
        1,
    )
    before = passed_along(tail, "seq", 1)
    projected = jnp.concatenate([project(normed, w) for w in (w_query, w_key)], 1)
    v_raw = project_heads(normed, w_value)
    z_heads = project_heads(normed, w_zgate)
    width_q = w_query.shape[1]
    width_k = w_key.shape[1]
    split_at = width_q + width_k
    extended = jnp.concatenate([before[:, :split_at], projected], 0).astype(jnp.float32)
    conv_out = conv_all[0] * extended[0:length]
    for index in range(1, taps):
        conv_out = conv_out + conv_all[index] * extended[index : index + length]
    conv_out = jax.nn.silu(conv_out)
    before_v = before[:, split_at:].reshape(taps - 1, value_heads, DV).transpose(1, 0, 2)
    extended_v = jnp.concatenate([before_v, v_raw], 1).astype(jnp.float32)
    taps_v = conv_value.reshape(taps, value_heads, 1, DV)
    conv_v = taps_v[0] * extended_v[:, 0:length]
    for index in range(1, taps):
        conv_v = conv_v + taps_v[index] * extended_v[:, index : index + length]
    conv_v = jax.nn.silu(conv_v)
    key_heads = width_q // DK
    group = value_heads // key_heads
    query = unit_heads(conv_out[:, :width_q], key_heads) * DK ** (-0.5)
    keyvec = unit_heads(conv_out[:, width_q : width_q + width_k], key_heads)
    query = jnp.repeat(query, group, axis=1)
    keyvec = jnp.repeat(keyvec, group, axis=1)
    blocks = length // STRETCH

    def by_block(array):
        return array.reshape(blocks, STRETCH, value_heads, -1).transpose(2, 0, 1, 3)

    q_blk = by_block(query)
    k_blk = by_block(keyvec)
    v_blk = conv_v.reshape(value_heads, blocks, STRETCH, DV)
    g_blk = log_decay.reshape(blocks, STRETCH, value_heads).transpose(2, 0, 1)
    b_blk = write_rate.reshape(blocks, STRETCH, value_heads).transpose(2, 0, 1)
    cumul = jnp.cumsum(g_blk, -1)
    last_cum = cumul[..., -1:]
    places = jnp.arange(STRETCH)
    lower_incl = places[:, None] >= places[None, :]
    lower_strict = places[:, None] > places[None, :]
    spread_log = cumul[..., :, None] - cumul[..., None, :]
    ratio_incl = jnp.where(lower_incl, jnp.exp(jnp.where(lower_incl, spread_log, 0.0)), 0.0)
    key_gram = mix("hnid,hnjd->hnij", k_blk, k_blk)
    strict = jnp.where(lower_strict, b_blk[..., None] * key_gram * ratio_incl, 0.0)
    inverse = unit_lower_inverse(strict)
    decay_in = jnp.exp(cumul)[..., None]
    right_side = jnp.concatenate(
        [b_blk[..., None] * decay_in * k_blk, b_blk[..., None] * v_blk], -1
    )
    solved = mix("hnij,hnjc->hnic", inverse, right_side)
    w_mat = solved[..., :DK]
    u_mat = solved[..., DK:]
    key_tail = k_blk * jnp.exp(last_cum - cumul)[..., None]
    eye_key = jnp.eye(DK, dtype=jnp.float32)
    transit = jnp.exp(last_cum)[..., None] * eye_key - mix("hnik,hnil->hnkl", w_mat, key_tail)
    inject = mix("hniv,hnik->hnvk", u_mat, key_tail)
    total_map, total_add = block_total(transit, inject)
    incoming = shard_prefix(total_map, total_add)
    map_incl, add_incl = block_prefix(transit, inject)
    ident_maps = jnp.broadcast_to(eye_key, (value_heads, 1, DK, DK))
    zero_add = jnp.zeros((value_heads, 1, DV, DK), jnp.float32)
    map_prefix = jnp.concatenate([ident_maps, map_incl[:, :-1]], 1)
    add_prefix = jnp.concatenate([zero_add, add_incl[:, :-1]], 1)
    scores = mix("hnid,hnjd->hnij", q_blk, k_blk) * ratio_incl
    reach = decay_in * q_blk - mix("hnij,hnjk->hnik", scores, w_mat)
    carried = mix("hnik,hnlk->hnil", reach, map_prefix)
    local = mix("hnik,hnvk->hniv", reach, add_prefix) + mix("hnij,hnjv->hniv", scores, u_mat)
    out_blk = mix("hnil,hvl->hniv", carried, incoming) + local
    delta_out = out_blk.reshape(value_heads, length, DV)
    gate_z = z_heads.astype(jnp.float32)
    gated = (rms_scale(delta_out, norm_gain) * jax.nn.silu(gate_z)).astype(jnp.bfloat16)
    n_exp = lax.axis_size("exp")
    row_share = length // n_exp
    gated = lax.optimization_barrier(gated)
    attn_rows = lax.psum_scatter(
        jnp.einsum(
            "htv,hvd->td",
            gated,
            w_out.reshape(value_heads, DV, -1),
            preferred_element_type=jnp.float32,
        ).astype(jnp.bfloat16),
        "exp",
        scatter_dimension=0,
        tiled=True,
    ).astype(jnp.float32)
    own_rows = lax.dynamic_slice_in_dim(
        whole, lax.axis_index("exp") * row_share, row_share, 0
    ).astype(jnp.float32)
    resid = own_rows + attn_rows
    post = rms_scale(resid, post_gain).astype(jnp.bfloat16)
    topk = expert_ids.shape[1]
    experts = w_gate.shape[0] * n_exp
    capacity = 2 * row_share * topk // experts
    flat_ids = expert_ids.reshape(-1)
    hits = (flat_ids[:, None] == jnp.arange(experts)[None, :]).astype(jnp.int32)
    earlier_hits = jnp.cumsum(hits, 0) - hits
    slot_of = jnp.sum(earlier_hits * hits, 1)
    target = flat_ids * capacity + slot_of
    route_map = (target[:, None] == jnp.arange(experts * capacity)[None, :]).astype(jnp.bfloat16)
    spread_rows = jnp.repeat(post, topk, axis=0)
    outgoing = jnp.einsum(
        "rp,rd->pd", route_map, spread_rows, preferred_element_type=jnp.float32
    ).astype(jnp.bfloat16)
    outgoing = outgoing.reshape(experts, 1, capacity, post.shape[1])
    batch = lax.all_to_all(outgoing, "exp", split_axis=0, concat_axis=1, tiled=True)
    gate_v = jnp.einsum("esnd,edf->esnf", batch, w_gate, preferred_element_type=jnp.float32)
    up_v = jnp.einsum("esnd,edf->esnf", batch, w_up, preferred_element_type=jnp.float32)
    act = (jax.nn.silu(gate_v) * up_v).astype(jnp.bfloat16)
    processed = jnp.einsum(
        "esnf,efd->esnd", act, w_down, preferred_element_type=jnp.float32
    ).astype(jnp.bfloat16)
    returned = lax.all_to_all(processed, "exp", split_axis=1, concat_axis=0, tiled=True)
    flat_back = returned.reshape(experts * capacity, post.shape[1])
    fetched = jnp.dot(route_map, flat_back, preferred_element_type=jnp.float32).reshape(
        row_share, topk, post.shape[1]
    )
    moe_sum = jnp.sum(route_weight[..., None] * fetched, 1)
    return (resid + moe_sum).astype(jnp.bfloat16)


def solution(mesh):
    return jax.shard_map(
        per_device,
        mesh=mesh,
        in_specs=(
            P("seq", "exp"),
            P(),
            P(None, "exp"),
            P(None, "exp"),
            P(None, "exp"),
            P(None, "exp"),
            P(None, "exp"),
            P(None, "exp"),
            P(None, "exp"),
            P("seq", "exp"),
            P("seq", "exp"),
            P(),
            P("exp", None),
            P(),
            P(("seq", "exp"), None),
            P(("seq", "exp"), None),
            P("exp", None, None),
            P("exp", None, None),
            P("exp", None, None),
        ),
        out_specs=P(("seq", "exp"), None),
        check_vma=False,
    )
```

```python
import jax
import jax.numpy as jnp
from jax import lax
from jax.sharding import PartitionSpec as P

DK = 128
DV = 128
STRETCH = 64
RADIX = 4


EPS = 1e-06
HIGH = lax.Precision.HIGH


def passed_along(block, axis, distance):
    devices = range(lax.axis_size(axis))
    route = [(i - distance, i) for i in devices if i - distance in devices]
    return lax.ppermute(block, axis, route)


def rms_scale(values, gain):
    return values * lax.rsqrt(jnp.mean(values * values, -1, keepdims=True) + EPS) * gain


def mix(form, left_arr, right_arr):
    return jnp.einsum(form, left_arr, right_arr, precision=HIGH)


def unit_heads(values, heads):
    shaped = values.reshape(values.shape[0], heads, -1)
    return shaped * lax.rsqrt(jnp.sum(shaped * shaped, -1, keepdims=True) + EPS)


def unit_lower_inverse(strict):
    size = strict.shape[-1]
    rows = lax.broadcasted_iota(jnp.int32, (size, size), 0)
    cols = lax.broadcasted_iota(jnp.int32, (size, size), 1)
    inverse = jnp.broadcast_to(jnp.eye(size, dtype=strict.dtype), strict.shape)
    span = 1
    while span < size:
        pick = (
            (rows // (2 * span) == cols // (2 * span))
            & ((rows // span) % 2 == 1)
            & ((cols // span) % 2 == 0)
        )
        coupling = jnp.where(pick, strict, 0.0)
        spread = lax.optimization_barrier(mix("...ij,...jk->...ik", coupling, inverse))
        inverse = inverse - lax.optimization_barrier(mix("...ij,...jk->...ik", inverse, spread))
        span *= 2
    return inverse


def compose(first_map, first_add, then_map, then_add):
    stacked = jnp.concatenate([first_map, first_add], -2)
    moved = mix("...kl,...lm->...km", stacked, then_map)
    rows = first_map.shape[-2]
    return moved[..., :rows, :], moved[..., rows:, :] + then_add


def block_prefix(maps, adds):
    count = maps.shape[1]
    eye = jnp.eye(maps.shape[-1], dtype=maps.dtype)
    shift = 1
    while shift < count:
        pad_map = jnp.broadcast_to(eye, maps[:, :shift].shape)
        pad_add = jnp.zeros_like(adds[:, :shift])
        prev_map = jnp.concatenate([pad_map, maps[:, :-shift]], 1)
        prev_add = jnp.concatenate([pad_add, adds[:, :-shift]], 1)
        maps, adds = compose(prev_map, prev_add, maps, adds)
        shift *= 2
    return maps, adds


def block_total(maps, adds):
    while maps.shape[1] > 1:
        paired_maps = maps.reshape(maps.shape[0], -1, 2, *maps.shape[2:])
        paired_adds = adds.reshape(adds.shape[0], -1, 2, *adds.shape[2:])
        maps, adds = compose(
            paired_maps[:, :, 0], paired_adds[:, :, 0], paired_maps[:, :, 1], paired_adds[:, :, 1]
        )
    return maps[:, 0], adds[:, 0]


def shard_prefix(total_map, total_add):
    place = lax.axis_index("seq")
    packed = jnp.stack([total_map, total_add]).astype(jnp.bfloat16)
    gathered = lax.all_gather(packed, "seq").astype(total_map.dtype)
    earlier = (jnp.arange(gathered.shape[0]) < place)[:, None, None, None]
    eye = jnp.eye(total_map.shape[-1], dtype=total_map.dtype)
    maps = jnp.where(earlier, gathered[:, 0], eye)
    adds = jnp.where(earlier, gathered[:, 1], 0.0)
    while maps.shape[0] > 1:
        paired_maps = maps.reshape(-1, 2, *maps.shape[1:])
        paired_adds = adds.reshape(-1, 2, *adds.shape[1:])
        maps, adds = compose(
            paired_maps[:, 0], paired_adds[:, 0], paired_maps[:, 1], paired_adds[:, 1]
        )
    return adds[0]


def per_device(
    tokens,
    in_gain,
    w_query,
    w_key,
    w_value,
    w_zgate,
    conv_query,
    conv_key,
    conv_value,
    log_decay,
    write_rate,
    norm_gain,
    w_out,
    post_gain,
    expert_ids,
    route_weight,
    w_gate,
    w_up,
    w_down,
):
    whole = lax.all_gather(tokens, "exp", axis=1, tiled=True)
    x_float = whole.astype(jnp.float32)
    normed = rms_scale(x_float, in_gain).astype(jnp.bfloat16)

    def project(rows, weight):
        return jnp.dot(rows, weight, preferred_element_type=jnp.float32).astype(jnp.bfloat16)

    value_heads = w_value.shape[1] // DV

    def project_heads(rows, weight):
        split = weight.reshape(weight.shape[0], value_heads, -1)
        return jnp.einsum(
            "td,dhe->hte", rows, split, preferred_element_type=jnp.float32
        ).astype(jnp.bfloat16)

    conv_all = jnp.concatenate([conv_query, conv_key], 1)
    taps = conv_all.shape[0]
    length = normed.shape[0]
    last_rows = normed[length - (taps - 1) :]
    tail_v = project_heads(last_rows, w_value)
    tail = jnp.concatenate(
        [project(last_rows, w) for w in (w_query, w_key)]
        + [tail_v.transpose(1, 0, 2).reshape(taps - 1, -1)],
        1,
    )
    before = passed_along(tail, "seq", 1)
    projected = jnp.concatenate([project(normed, w) for w in (w_query, w_key)], 1)
    v_raw = project_heads(normed, w_value)
    z_heads = project_heads(normed, w_zgate)
    width_q = w_query.shape[1]
    width_k = w_key.shape[1]
    split_at = width_q + width_k
    extended = jnp.concatenate([before[:, :split_at], projected], 0).astype(jnp.float32)
    conv_out = conv_all[0] * extended[0:length]
    for index in range(1, taps):
        conv_out = conv_out + conv_all[index] * extended[index : index + length]
    conv_out = jax.nn.silu(conv_out)
    before_v = before[:, split_at:].reshape(taps - 1, value_heads, DV).transpose(1, 0, 2)
    extended_v = jnp.concatenate([before_v, v_raw], 1).astype(jnp.float32)
    taps_v = conv_value.reshape(taps, value_heads, 1, DV)
    conv_v = taps_v[0] * extended_v[:, 0:length]
    for index in range(1, taps):
        conv_v = conv_v + taps_v[index] * extended_v[:, index : index + length]
    conv_v = jax.nn.silu(conv_v)
    key_heads = width_q // DK
    group = value_heads // key_heads
    query = unit_heads(conv_out[:, :width_q], key_heads) * DK ** (-0.5)
    keyvec = unit_heads(conv_out[:, width_q : width_q + width_k], key_heads)
    query = jnp.repeat(query, group, axis=1)
    keyvec = jnp.repeat(keyvec, group, axis=1)
    blocks = length // STRETCH

    def by_block(array):
        return array.reshape(blocks, STRETCH, value_heads, -1).transpose(2, 0, 1, 3)

    q_blk = by_block(query)
    k_blk = by_block(keyvec)
    v_blk = conv_v.reshape(value_heads, blocks, STRETCH, DV)
    g_blk = log_decay.reshape(blocks, STRETCH, value_heads).transpose(2, 0, 1)
    b_blk = write_rate.reshape(blocks, STRETCH, value_heads).transpose(2, 0, 1)
    cumul = jnp.cumsum(g_blk, -1)
    last_cum = cumul[..., -1:]
    places = jnp.arange(STRETCH)
    lower_incl = places[:, None] >= places[None, :]
    lower_strict = places[:, None] > places[None, :]
    spread_log = cumul[..., :, None] - cumul[..., None, :]
    ratio_incl = jnp.where(lower_incl, jnp.exp(jnp.where(lower_incl, spread_log, 0.0)), 0.0)
    key_gram = mix("hnid,hnjd->hnij", k_blk, k_blk)
    strict = jnp.where(lower_strict, b_blk[..., None] * key_gram * ratio_incl, 0.0)
    inverse = unit_lower_inverse(strict)
    decay_in = jnp.exp(cumul)[..., None]
    right_side = jnp.concatenate(
        [b_blk[..., None] * decay_in * k_blk, b_blk[..., None] * v_blk], -1
    )
    solved = mix("hnij,hnjc->hnic", inverse, right_side)
    w_mat = solved[..., :DK]
    u_mat = solved[..., DK:]
    key_tail = k_blk * jnp.exp(last_cum - cumul)[..., None]
    eye_key = jnp.eye(DK, dtype=jnp.float32)
    transit = jnp.exp(last_cum)[..., None] * eye_key - mix("hnik,hnil->hnkl", w_mat, key_tail)
    inject = mix("hniv,hnik->hnvk", u_mat, key_tail)
    total_map, total_add = block_total(transit, inject)
    incoming = shard_prefix(total_map, total_add)
    map_incl, add_incl = block_prefix(transit, inject)
    ident_maps = jnp.broadcast_to(eye_key, (value_heads, 1, DK, DK))
    zero_add = jnp.zeros((value_heads, 1, DV, DK), jnp.float32)
    map_prefix = jnp.concatenate([ident_maps, map_incl[:, :-1]], 1)
    add_prefix = jnp.concatenate([zero_add, add_incl[:, :-1]], 1)
    scores = mix("hnid,hnjd->hnij", q_blk, k_blk) * ratio_incl
    reach = decay_in * q_blk - mix("hnij,hnjk->hnik", scores, w_mat)
    carried = mix("hnik,hnlk->hnil", reach, map_prefix)
    local = mix("hnik,hnvk->hniv", reach, add_prefix) + mix("hnij,hnjv->hniv", scores, u_mat)
    out_blk = mix("hnil,hvl->hniv", carried, incoming) + local
    delta_out = out_blk.reshape(value_heads, length, DV)
    gate_z = z_heads.astype(jnp.float32)
    gated = (rms_scale(delta_out, norm_gain) * jax.nn.silu(gate_z)).astype(jnp.bfloat16)
    n_exp = lax.axis_size("exp")
    row_share = length // n_exp
    gated = lax.optimization_barrier(gated)
    attn_rows = lax.psum_scatter(
        jnp.einsum(
            "htv,hvd->td",
            gated,
            w_out.reshape(value_heads, DV, -1),
            preferred_element_type=jnp.float32,
        ).astype(jnp.bfloat16),
        "exp",
        scatter_dimension=0,
        tiled=True,
    ).astype(jnp.float32)
    own_rows = lax.dynamic_slice_in_dim(
        whole, lax.axis_index("exp") * row_share, row_share, 0
    ).astype(jnp.float32)
    resid = own_rows + attn_rows
    post = rms_scale(resid, post_gain).astype(jnp.bfloat16)
    topk = expert_ids.shape[1]
    experts = w_gate.shape[0] * n_exp
    capacity = 2 * row_share * topk // experts
    flat_ids = expert_ids.reshape(-1)
    hits = (flat_ids[:, None] == jnp.arange(experts)[None, :]).astype(jnp.int32)
    earlier_hits = jnp.cumsum(hits, 0) - hits
    slot_of = jnp.sum(earlier_hits * hits, 1)
    target = flat_ids * capacity + slot_of
    route_map = (target[:, None] == jnp.arange(experts * capacity)[None, :]).astype(jnp.bfloat16)
    spread_rows = jnp.repeat(post, topk, axis=0)
    outgoing = jnp.einsum(
        "rp,rd->pd", route_map, spread_rows, preferred_element_type=jnp.float32
    ).astype(jnp.bfloat16)
    outgoing = outgoing.reshape(experts, 1, capacity, post.shape[1])
    batch = lax.all_to_all(outgoing, "exp", split_axis=0, concat_axis=1, tiled=True)
    gate_v = jnp.einsum("esnd,edf->esnf", batch, w_gate, preferred_element_type=jnp.float32)
    up_v = jnp.einsum("esnd,edf->esnf", batch, w_up, preferred_element_type=jnp.float32)
    act = (jax.nn.silu(gate_v) * up_v).astype(jnp.bfloat16)
    processed = jnp.einsum(
        "esnf,efd->esnd", act, w_down, preferred_element_type=jnp.float32
    ).astype(jnp.bfloat16)
    returned = lax.all_to_all(processed, "exp", split_axis=1, concat_axis=0, tiled=True)
    flat_back = returned.reshape(experts * capacity, post.shape[1])
    fetched = jnp.dot(route_map, flat_back, preferred_element_type=jnp.float32).reshape(
        row_share, topk, post.shape[1]
    )
    moe_sum = jnp.sum(route_weight[..., None] * fetched, 1)
    return (resid + moe_sum).astype(jnp.bfloat16)


def solution(mesh):
    return jax.shard_map(
        per_device,
        mesh=mesh,
        in_specs=(
            P("seq", "exp"),
            P(),
            P(None, "exp"),
            P(None, "exp"),
            P(None, "exp"),
            P(None, "exp"),
            P(None, "exp"),
            P(None, "exp"),
            P(None, "exp"),
            P("seq", "exp"),
            P("seq", "exp"),
            P(),
            P("exp", None),
            P(),
            P(("seq", "exp"), None),
            P(("seq", "exp"), None),
            P("exp", None, None),
            P("exp", None, None),
            P("exp", None, None),
        ),
        out_specs=P(("seq", "exp"), None),
        check_vma=False,
    )
```

```python
import jax
import jax.numpy as jnp
from jax import lax
from jax.sharding import PartitionSpec as P

DK = 128
DV = 128
STRETCH = 64
RADIX = 4


EPS = 1e-06
HIGH = lax.Precision.HIGH


def passed_along(block, axis, distance):
    devices = range(lax.axis_size(axis))
    route = [(i - distance, i) for i in devices if i - distance in devices]
    return lax.ppermute(block, axis, route)


def rms_scale(values, gain):
    return values * lax.rsqrt(jnp.mean(values * values, -1, keepdims=True) + EPS) * gain


def mix(form, left_arr, right_arr):
    return jnp.einsum(form, left_arr, right_arr, precision=HIGH)


def unit_heads(values, heads):
    shaped = values.reshape(values.shape[0], heads, -1)
    return shaped * lax.rsqrt(jnp.sum(shaped * shaped, -1, keepdims=True) + EPS)


def unit_lower_inverse(strict):
    size = strict.shape[-1]
    rows = lax.broadcasted_iota(jnp.int32, (size, size), 0)
    cols = lax.broadcasted_iota(jnp.int32, (size, size), 1)
    inverse = jnp.broadcast_to(jnp.eye(size, dtype=strict.dtype), strict.shape)
    span = 1
    while span < size:
        pick = (
            (rows // (2 * span) == cols // (2 * span))
            & ((rows // span) % 2 == 1)
            & ((cols // span) % 2 == 0)
        )
        coupling = jnp.where(pick, strict, 0.0)
        spread = lax.optimization_barrier(mix("...ij,...jk->...ik", coupling, inverse))
        inverse = inverse - lax.optimization_barrier(mix("...ij,...jk->...ik", inverse, spread))
        span *= 2
    return inverse


def compose(first_map, first_add, then_map, then_add):
    stacked = jnp.concatenate([first_map, first_add], -2)
    moved = mix("...kl,...lm->...km", stacked, then_map)
    rows = first_map.shape[-2]
    return moved[..., :rows, :], moved[..., rows:, :] + then_add


def block_prefix(maps, adds):
    count = maps.shape[1]
    eye = jnp.eye(maps.shape[-1], dtype=maps.dtype)
    shift = 1
    while shift < count:
        pad_map = jnp.broadcast_to(eye, maps[:, :shift].shape)
        pad_add = jnp.zeros_like(adds[:, :shift])
        prev_map = jnp.concatenate([pad_map, maps[:, :-shift]], 1)
        prev_add = jnp.concatenate([pad_add, adds[:, :-shift]], 1)
        maps, adds = compose(prev_map, prev_add, maps, adds)
        shift *= 2
    return maps, adds


def block_total(maps, adds):
    while maps.shape[1] > 1:
        maps, adds = compose(maps[:, 0::2], adds[:, 0::2], maps[:, 1::2], adds[:, 1::2])
    return maps[:, 0], adds[:, 0]


def shard_prefix(total_map, total_add):
    place = lax.axis_index("seq")
    rows = total_map.shape[-2]
    packed = jnp.concatenate([total_map, total_add], -2).astype(jnp.bfloat16)
    gathered = lax.all_gather(packed, "seq").astype(total_map.dtype)
    earlier = (jnp.arange(gathered.shape[0]) < place)[:, None, None, None]
    eye = jnp.eye(total_map.shape[-1], dtype=total_map.dtype)
    ident = jnp.concatenate([eye, jnp.zeros_like(eye)], 0)
    pairs = jnp.where(earlier, gathered, ident)
    while pairs.shape[0] > 1:
        split = pairs.reshape(-1, 2, *pairs.shape[1:])
        first, then = split[:, 0], split[:, 1]
        moved = mix("...kl,...lm->...km", first, then[..., :rows, :])
        pairs = jnp.concatenate([moved[..., :rows, :], moved[..., rows:, :] + then[..., rows:, :]], -2)
    return pairs[0][..., rows:, :]


def per_device(
    tokens,
    in_gain,
    w_query,
    w_key,
    w_value,
    w_zgate,
    conv_query,
    conv_key,
    conv_value,
    log_decay,
    write_rate,
    norm_gain,
    w_out,
    post_gain,
    expert_ids,
    route_weight,
    w_gate,
    w_up,
    w_down,
):
    whole = lax.all_gather(tokens, "exp", axis=1, tiled=True)
    x_float = whole.astype(jnp.float32)
    normed = rms_scale(x_float, in_gain).astype(jnp.bfloat16)

    def project(rows, weight):
        return jnp.dot(rows, weight, preferred_element_type=jnp.float32).astype(jnp.bfloat16)

    value_heads = w_value.shape[1] // DV

    def project_heads(rows, weight):
        split = weight.reshape(weight.shape[0], value_heads, -1)
        return jnp.einsum(
            "td,dhe->hte", rows, split, preferred_element_type=jnp.float32
        ).astype(jnp.bfloat16)

    conv_all = jnp.concatenate([conv_query, conv_key], 1)
    taps = conv_all.shape[0]
    length = normed.shape[0]
    last_rows = normed[length - (taps - 1) :]
    tail_v = project_heads(last_rows, w_value)
    tail = jnp.concatenate(
        [project(last_rows, w) for w in (w_query, w_key)]
        + [tail_v.transpose(1, 0, 2).reshape(taps - 1, -1)],
        1,
    )
    before = passed_along(tail, "seq", 1)
    projected = jnp.concatenate([project(normed, w) for w in (w_query, w_key)], 1)
    v_raw = project_heads(normed, w_value)
    z_heads = project_heads(normed, w_zgate)
    width_q = w_query.shape[1]
    width_k = w_key.shape[1]
    split_at = width_q + width_k
    extended = jnp.concatenate([before[:, :split_at], projected], 0).astype(jnp.float32)
    conv_out = conv_all[0] * extended[0:length]
    for index in range(1, taps):
        conv_out = conv_out + conv_all[index] * extended[index : index + length]
    conv_out = jax.nn.silu(conv_out)
    before_v = before[:, split_at:].reshape(taps - 1, value_heads, DV).transpose(1, 0, 2)
    extended_v = jnp.concatenate([before_v, v_raw], 1).astype(jnp.float32)
    taps_v = conv_value.reshape(taps, value_heads, 1, DV)
    conv_v = taps_v[0] * extended_v[:, 0:length]
    for index in range(1, taps):
        conv_v = conv_v + taps_v[index] * extended_v[:, index : index + length]
    conv_v = jax.nn.silu(conv_v)
    key_heads = width_q // DK
    group = value_heads // key_heads
    query = unit_heads(conv_out[:, :width_q], key_heads) * DK ** (-0.5)
    keyvec = unit_heads(conv_out[:, width_q : width_q + width_k], key_heads)
    query = jnp.repeat(query, group, axis=1)
    keyvec = jnp.repeat(keyvec, group, axis=1)
    blocks = length // STRETCH

    def by_block(array):
        return array.reshape(blocks, STRETCH, value_heads, -1).transpose(2, 0, 1, 3)

    q_blk = by_block(query)
    k_blk = by_block(keyvec)
    v_blk = conv_v.reshape(value_heads, blocks, STRETCH, DV)
    g_blk = log_decay.reshape(blocks, STRETCH, value_heads).transpose(2, 0, 1)
    b_blk = write_rate.reshape(blocks, STRETCH, value_heads).transpose(2, 0, 1)
    cumul = jnp.cumsum(g_blk, -1)
    last_cum = cumul[..., -1:]
    places = jnp.arange(STRETCH)
    lower_incl = places[:, None] >= places[None, :]
    lower_strict = places[:, None] > places[None, :]
    spread_log = cumul[..., :, None] - cumul[..., None, :]
    ratio_incl = jnp.where(lower_incl, jnp.exp(jnp.where(lower_incl, spread_log, 0.0)), 0.0)
    key_gram = mix("hnid,hnjd->hnij", k_blk, k_blk)
    strict = jnp.where(lower_strict, b_blk[..., None] * key_gram * ratio_incl, 0.0)
    inverse = unit_lower_inverse(strict)
    decay_in = jnp.exp(cumul)[..., None]
    right_side = jnp.concatenate(
        [b_blk[..., None] * decay_in * k_blk, b_blk[..., None] * v_blk], -1
    )
    solved = mix("hnij,hnjc->hnic", inverse, right_side)
    w_mat = solved[..., :DK]
    u_mat = solved[..., DK:]
    key_tail = k_blk * jnp.exp(last_cum - cumul)[..., None]
    eye_key = jnp.eye(DK, dtype=jnp.float32)
    transit = jnp.exp(last_cum)[..., None] * eye_key - mix("hnik,hnil->hnkl", w_mat, key_tail)
    inject = mix("hniv,hnik->hnvk", u_mat, key_tail)
    total_map, total_add = block_total(transit, inject)
    incoming = shard_prefix(total_map, total_add)
    map_incl, add_incl = block_prefix(transit, inject)
    ident_maps = jnp.broadcast_to(eye_key, (value_heads, 1, DK, DK))
    zero_add = jnp.zeros((value_heads, 1, DV, DK), jnp.float32)
    map_prefix = jnp.concatenate([ident_maps, map_incl[:, :-1]], 1)
    add_prefix = jnp.concatenate([zero_add, add_incl[:, :-1]], 1)
    scores = mix("hnid,hnjd->hnij", q_blk, k_blk) * ratio_incl
    reach = decay_in * q_blk - mix("hnij,hnjk->hnik", scores, w_mat)
    carried = mix("hnik,hnlk->hnil", reach, map_prefix)
    local = mix("hnik,hnvk->hniv", reach, add_prefix) + mix("hnij,hnjv->hniv", scores, u_mat)
    out_blk = mix("hnil,hvl->hniv", carried, incoming) + local
    delta_out = out_blk.reshape(value_heads, length, DV)
    gate_z = z_heads.astype(jnp.float32)
    gated = (rms_scale(delta_out, norm_gain) * jax.nn.silu(gate_z)).astype(jnp.bfloat16)
    n_exp = lax.axis_size("exp")
    row_share = length // n_exp
    gated = lax.optimization_barrier(gated)
    attn_rows = lax.psum_scatter(
        jnp.einsum(
            "htv,hvd->td",
            gated,
            w_out.reshape(value_heads, DV, -1),
            preferred_element_type=jnp.float32,
        ).astype(jnp.bfloat16),
        "exp",
        scatter_dimension=0,
        tiled=True,
    ).astype(jnp.float32)
    own_rows = lax.dynamic_slice_in_dim(
        whole, lax.axis_index("exp") * row_share, row_share, 0
    ).astype(jnp.float32)
    resid = own_rows + attn_rows
    post = rms_scale(resid, post_gain).astype(jnp.bfloat16)
    topk = expert_ids.shape[1]
    experts = w_gate.shape[0] * n_exp
    capacity = 2 * row_share * topk // experts
    flat_ids = expert_ids.reshape(-1)
    hits = (flat_ids[:, None] == jnp.arange(experts)[None, :]).astype(jnp.int32)
    earlier_hits = jnp.cumsum(hits, 0) - hits
    slot_of = jnp.sum(earlier_hits * hits, 1)
    target = flat_ids * capacity + slot_of
    route_map = (target[:, None] == jnp.arange(experts * capacity)[None, :]).astype(jnp.bfloat16)
    spread_rows = jnp.repeat(post, topk, axis=0)
    outgoing = jnp.einsum(
        "rp,rd->pd", route_map, spread_rows, preferred_element_type=jnp.float32
    ).astype(jnp.bfloat16)
    outgoing = outgoing.reshape(experts, 1, capacity, post.shape[1])
    batch = lax.all_to_all(outgoing, "exp", split_axis=0, concat_axis=1, tiled=True)
    gate_v = jnp.einsum("esnd,edf->esnf", batch, w_gate, preferred_element_type=jnp.float32)
    up_v = jnp.einsum("esnd,edf->esnf", batch, w_up, preferred_element_type=jnp.float32)
    act = (jax.nn.silu(gate_v) * up_v).astype(jnp.bfloat16)
    processed = jnp.einsum(
        "esnf,efd->esnd", act, w_down, preferred_element_type=jnp.float32
    ).astype(jnp.bfloat16)
    returned = lax.all_to_all(processed, "exp", split_axis=1, concat_axis=0, tiled=True)
    flat_back = returned.reshape(experts * capacity, post.shape[1])
    fetched = jnp.dot(route_map, flat_back, preferred_element_type=jnp.float32).reshape(
        row_share, topk, post.shape[1]
    )
    moe_sum = jnp.sum(route_weight[..., None] * fetched, 1)
    return (resid + moe_sum).astype(jnp.bfloat16)


def solution(mesh):
    return jax.shard_map(
        per_device,
        mesh=mesh,
        in_specs=(
            P("seq", "exp"),
            P(),
            P(None, "exp"),
            P(None, "exp"),
            P(None, "exp"),
            P(None, "exp"),
            P(None, "exp"),
            P(None, "exp"),
            P(None, "exp"),
            P("seq", "exp"),
            P("seq", "exp"),
            P(),
            P("exp", None),
            P(),
            P(("seq", "exp"), None),
            P(("seq", "exp"), None),
            P("exp", None, None),
            P("exp", None, None),
            P("exp", None, None),
        ),
        out_specs=P(("seq", "exp"), None),
        check_vma=False,
    )
```
